128 devices in a mesh: dp: 4 (over x), ctx: 8 (over z, core), head: 4 (over y).
Axes of the slice: x: 4, y: 4, z: 4, core: 2. Of those that a mesh axis runs over, the one named last changes fastest.
Arguments:
- token_values: bfloat16 [4, 4096, 8192], P('dp', 'ctx', 'head'), may hold values from -6 to 6
- gate_values: bfloat16 [4, 4096, 8192], P('dp', 'ctx', 'head'), may hold values from -6 to 6
- state_maps: bfloat16 [4, 4096, 8, 512], P('dp', 'ctx', 'head'), may hold values from -6 to 6
- step_raw: bfloat16 [4, 4096, 128], P('dp', 'ctx', 'head'), may hold values from -6.7 to 9.683792
- log_rate: float32 [128], P('head'), may hold values from -6 to 3
- skip_gain: float32 [128], P('head'), may hold values from 0.5 to 1.5
- conv_values: float32 [4, 8192], P(None, 'head'), may hold values from -3 to 3
- conv_maps: float32 [4, 8, 512], P(None, 'head'), may hold values from -3 to 3
- piece_shift: int32 [32], replicated, may hold values from 0 to 31, as said below
- doc_start: int32 [4, 4096], P('dp', 'ctx'), may hold values 0 or 1
- norm_gain: float32 [8192], P('head'), may hold values from 0.1 to 1.9
- out_weight: bfloat16 [8192, 4096], P('head'), may hold values from -0.0625 to 0.0625
Outputs:
- mixed: bfloat16 [4, 4096, 4096], P('dp', 'ctx', 'head')
The draws below stay inside these ranges and needn't reach their ends.
Inputs may be any that keep to these rules, and one draw needn't show every extreme that they name: `piece_shift`: no value occurs more than 2 times and some value occurs exactly 2 times.
All inputs are finite; a program needn't handle non-finite values. No bound on the sum of `doc_start` on one device may be relied on, other than what follows from the above.
Results may differ from the reference program's by a relative error of at most 0.014.
Values may be sent and summed in bfloat16 or wider, within the bound.
No kernel may reach another device: no remote copies, remote signals or barrier semaphores. Data moves between devices by JAX's collectives and lax.ppermute only.
A program may use at most 256 MiB of HBM per device.

```python
import math
import jax
import jax.numpy as jnp
from jax import lax

D = 4096
HEADS = 128
HEAD_DIM = 64
STATE = 256
GROUPS = 8
KERNEL = 4
BLOCK_LEN = 128
PIECES_DEV = 32
TOK_DEV = 512
OWNERS = 32
MOST = 2
BUNDLE_SLOTCOUNT = 4096
INNER = 8192
N_DP = 4


def draw_log_rate(key, part):
    nominal_interval_width = math.log(1.0 + math.exp(-6.0))
    lookup_matrix_lines = jax.random.split(key, 3)
    share = 0.5
    slow = jax.random.uniform(lookup_matrix_lines[0], (HEADS,)) < share
    slow_rate = jax.random.uniform(lookup_matrix_lines[1], (HEADS,), minval=0.25, maxval=0.75) / (BUNDLE_SLOTCOUNT * nominal_interval_width)
    fast_rate = jax.random.uniform(lookup_matrix_lines[2], (HEADS,), minval=0.75, maxval=1.25) / (40.0 * nominal_interval_width)
    return jnp.log(jnp.where(slow, slow_rate, fast_rate)).astype(jnp.float32)


def draw_step_raw(key, part):
    nominal_interval_width = math.log(1.0 + math.exp(-6.0))
    spike_interval_width = 0.95 * BUNDLE_SLOTCOUNT * nominal_interval_width
    spike_amplitude = math.log(math.exp(spike_interval_width) - 1.0)
    lookup_matrix_lines = jax.random.split(key, 2)
    stochastic_perturbation = jax.random.uniform(lookup_matrix_lines[0], (N_DP, BUNDLE_SLOTCOUNT, HEADS), minval=-0.7, maxval=0.7)
    spike_occurrence = jax.random.uniform(lookup_matrix_lines[1], (N_DP, BUNDLE_SLOTCOUNT, 1)) < 2.0 / BUNDLE_SLOTCOUNT
    payload_matrix_lines = jnp.where(spike_occurrence, spike_amplitude, -6.0 + stochastic_perturbation)
    return payload_matrix_lines.astype(jnp.float32).astype(jnp.bfloat16)


def draw_piece_shift(key, part):
    lookup_matrix_lines = jax.random.split(key, 3)
    first = jax.random.randint(lookup_matrix_lines[0], (), 0, OWNERS)
    pool = jax.random.permutation(lookup_matrix_lines[1], OWNERS * MOST) // MOST
    scores = jnp.where(pool == first, 0, 1 + jnp.arange(OWNERS * MOST))
    ordered = pool[jnp.argsort(scores, stable=True)]
    picked = ordered[:PIECES_DEV]
    return jax.random.permutation(lookup_matrix_lines[2], picked).astype(jnp.int32)


def place_ends(values, rng, smallest, top_value):
    dims = values.shape
    place = [jax.random.randint(jax.random.fold_in(rng, axis), (), 0, dims[axis]) for axis in range(len(dims))]
    values = values.at[tuple(place)].set(smallest)
    longest = dims.index(max(dims))
    place[longest] = (place[longest] + 1) % dims[longest]
    return values.at[tuple(place)].set(top_value)


def block_levels(rng, shape, cuts, low, largest):
    def one(dim, parts):
        heights = jax.random.uniform(jax.random.fold_in(jax.random.fold_in(rng, 6), dim), (parts,), jnp.float32, low / len(cuts), largest / len(cuts))
        return jnp.repeat(jnp.exp(heights), shape[dim] // parts).reshape((-1,) + (1,) * (len(shape) - dim - 1))

    level = one(*cuts[0])
    for cut in cuts[1:]:
        level = level * one(*cut)
    return level


def normal_values(stream_key, shape, deviation, bound, cuts=(), kind=jnp.bfloat16):
    values = deviation * jax.random.normal(stream_key, shape, jnp.float32)
    if cuts:
        values = values * block_levels(stream_key, shape, cuts, -0.22, 0.18)
    return jnp.clip(values, -bound, bound).astype(kind)


def setup_inputs(seed: int = 0) -> dict:
    streams_of = jax.random.split(jax.random.key(seed), 13)
    token_values = normal_values(streams_of[0], (N_DP, BUNDLE_SLOTCOUNT, INNER), 1.0, 6.0, ((0, 4), (1, 8), (2, 4)))
    gate_values = normal_values(streams_of[1], (N_DP, BUNDLE_SLOTCOUNT, INNER), 1.0, 6.0, ((0, 4), (1, 8), (2, 4)))
    state_maps = normal_values(streams_of[2], (N_DP, BUNDLE_SLOTCOUNT, GROUPS, 2 * STATE), 1.0, 6.0, ((0, 4), (1, 8), (2, 4)))
    step_raw = draw_step_raw(jax.random.fold_in(streams_of[12], 71), 0)
    log_rate = draw_log_rate(jax.random.fold_in(streams_of[12], 71), 0)
    skip_gain = jnp.clip(0.5 + 1.0 * jax.random.uniform(streams_of[5], (HEADS,), jnp.float32) ** block_levels(streams_of[5], (HEADS,), ((0, 4),), -0.2, 0.2), 0.5, 1.5)
    conv_values = normal_values(streams_of[6], (KERNEL, INNER), KERNEL ** -0.5, 3.0, ((1, 4),), jnp.float32)
    conv_maps = normal_values(streams_of[7], (KERNEL, GROUPS, 2 * STATE), KERNEL ** -0.5, 3.0, ((1, 4),), jnp.float32)
    piece_shift = draw_piece_shift(jax.random.fold_in(streams_of[12], 71), 0)
    doc_start = place_ends((jax.random.randint(streams_of[9], (N_DP, BUNDLE_SLOTCOUNT), 0, BUNDLE_SLOTCOUNT) < 2).astype(jnp.int32), jax.random.fold_in(streams_of[9], 1), 0, 1)
    norm_gain = jnp.clip(1.0 + 0.18 * jax.random.normal(streams_of[10], (INNER,), jnp.float32), 0.1, 1.9)
    out_weight = normal_values(streams_of[11], (INNER, D), INNER ** -0.5, 0.0625, ((0, 4),))
    return {"token_values": token_values, "gate_values": gate_values, "state_maps": state_maps, "step_raw": step_raw, "log_rate": log_rate, "skip_gain": skip_gain, "conv_values": conv_values, "conv_maps": conv_maps, "piece_shift": piece_shift, "doc_start": doc_start, "norm_gain": norm_gain, "out_weight": out_weight}


eps = 1e-05
highest = lax.Precision.HIGHEST

def conv_core(ext_values, weight, free_ext, length):
    tap_count = weight.shape[0]
    summed = jnp.zeros((length,) + ext_values.shape[1:], jnp.float32)
    keeping = jnp.ones((length,), jnp.float32)
    bshape = (length,) + (1,) * (ext_values.ndim - 1)
    for back in range(tap_count):
        if back > 0:
            keeping = keeping * free_ext[tap_count - back:tap_count - back + length]
        sample = ext_values[tap_count - 1 - back:tap_count - 1 - back + length].astype(jnp.float32)
        summed = summed + weight[tap_count - 1 - back] * sample * keeping.reshape(bshape)
    return jax.nn.silu(summed).astype(jnp.bfloat16)

def conv_silu(payload_matrix_lines, weight, free_flags):
    tap_count = weight.shape[0]
    padded = jnp.concatenate([jnp.zeros((tap_count - 1,) + payload_matrix_lines.shape[1:], payload_matrix_lines.dtype), payload_matrix_lines])
    free_ext = jnp.concatenate([jnp.ones((tap_count - 1,), jnp.float32), free_flags])
    return conv_core(padded, weight, free_ext, payload_matrix_lines.shape[0])

def mix_group(payload_matrix_lines, gates, maps, steps, rates, skips, conv_v, conv_m, starts, gains):
    length = payload_matrix_lines.shape[0]
    heads_here = rates.shape[0]
    width = payload_matrix_lines.shape[1] // heads_here
    state = maps.shape[1] // 2
    blocks = length // BLOCK_LEN
    free_flags = 1.0 - starts.astype(jnp.float32)
    x_conv = conv_silu(payload_matrix_lines, conv_v, free_flags)
    map_conv = conv_silu(maps, conv_m, free_flags)
    step_dt = jax.nn.softplus(steps.astype(jnp.float32))
    log_decay = step_dt * (-jnp.exp(rates))[None, :]
    cum_t = jnp.cumsum(log_decay.reshape(blocks, BLOCK_LEN, heads_here), axis=1).transpose(0, 2, 1)
    dt_t = step_dt.reshape(blocks, BLOCK_LEN, heads_here).transpose(0, 2, 1)
    segment = jnp.cumsum(starts.reshape(blocks, BLOCK_LEN), axis=1)
    x_blocks = x_conv.reshape(blocks, BLOCK_LEN, heads_here, width).astype(jnp.float32)
    b_blocks = map_conv[:, :state].reshape(blocks, BLOCK_LEN, state).astype(jnp.float32)
    c_blocks = map_conv[:, state:].reshape(blocks, BLOCK_LEN, state).astype(jnp.float32)
    scores = jnp.einsum('bqn,bsn->bqs', c_blocks, b_blocks, precision=highest)
    later = jnp.arange(BLOCK_LEN)[:, None] >= jnp.arange(BLOCK_LEN)[None, :]
    allowed = later[None] & (segment[:, :, None] == segment[:, None, :])
    spread = cum_t[:, :, :, None] - cum_t[:, :, None, :]
    decay = jnp.exp(jnp.where(allowed[:, None], spread, -jnp.inf))
    weights = (decay * scores[:, None] * dt_t[:, :, None, :]).astype(jnp.bfloat16)
    y_diag = jnp.einsum('bhts,bshp->bthp', weights.astype(jnp.float32), x_blocks, precision=highest)
    same_end = (segment == segment[:, -1:]).astype(jnp.float32)
    carry_coef = jnp.exp(cum_t[:, :, -1:] - cum_t) * dt_t * same_end[:, None, :]
    x_weighted = (x_blocks * carry_coef.transpose(0, 2, 1)[..., None]).astype(jnp.bfloat16)
    block_states = jnp.einsum('bshp,bsn->bhpn', x_weighted.astype(jnp.float32), b_blocks, precision=highest)
    block_gates = jnp.exp(cum_t[:, :, -1]) * (segment[:, -1] == 0).astype(jnp.float32)[:, None]

    def advance(summed, item):
        gate_now, state_now = item
        return (gate_now[:, None, None] * summed + state_now, summed)
    unused, entering = lax.scan(advance, jnp.zeros((heads_here, width, state), jnp.float32), (block_gates, block_states))
    entering = entering.astype(jnp.bfloat16).astype(jnp.float32)
    y_off = jnp.einsum('bqn,bhpn->bqhp', c_blocks, entering, precision=highest)
    reach = (jnp.exp(cum_t) * (segment == 0).astype(jnp.float32)[:, None, :]).transpose(0, 2, 1)[..., None]
    mixed_y = y_diag + y_off * reach + skips[None, None, :, None] * x_blocks
    gated = mixed_y * jax.nn.silu(gates.astype(jnp.float32).reshape(blocks, BLOCK_LEN, heads_here, width))
    power = lax.optimization_barrier(jnp.mean(gated * gated, axis=(2, 3), keepdims=True))
    normed = gated * lax.rsqrt(power + eps) * gains.reshape(heads_here, width)
    return normed.astype(jnp.bfloat16).reshape(length, heads_here * width)

def reference(token_values, gate_values, state_maps, step_raw, log_rate, skip_gain, conv_values, conv_maps, piece_shift, doc_start, norm_gain, out_weight):
    source = (jnp.arange(OWNERS, dtype=jnp.int32)[:, None] - piece_shift[None, :]) % OWNERS
    slot_ids = jnp.arange(PIECES_DEV, dtype=jnp.int32)[None, :]

    def route(array):
        pieces = array.reshape((OWNERS, PIECES_DEV, TOK_DEV // PIECES_DEV) + array.shape[2:])
        return pieces[source, slot_ids].reshape(array.shape)
    per_group = HEADS // GROUPS
    inner_group = per_group * HEAD_DIM
    payload_matrix_lines = route(token_values).reshape(N_DP, BUNDLE_SLOTCOUNT, GROUPS, inner_group)
    gates = route(gate_values).reshape(N_DP, BUNDLE_SLOTCOUNT, GROUPS, inner_group)
    maps = route(state_maps)
    steps = route(step_raw).reshape(N_DP, BUNDLE_SLOTCOUNT, GROUPS, per_group)
    rates = log_rate.reshape(GROUPS, per_group)
    skips = skip_gain.reshape(GROUPS, per_group)
    conv_v = conv_values.reshape(KERNEL, GROUPS, inner_group)
    gains = norm_gain.reshape(GROUPS, inner_group)

    def one_item(index):
        pack = index // GROUPS
        group = index % GROUPS
        return mix_group(payload_matrix_lines[pack, :, group], gates[pack, :, group], maps[pack, :, group], steps[pack, :, group], rates[group], skips[group], conv_v[:, group], conv_maps[:, group], doc_start[pack], gains[group])
    normed = lax.map(one_item, jnp.arange(N_DP * GROUPS, dtype=jnp.int32))
    normed = normed.reshape(N_DP, GROUPS, BUNDLE_SLOTCOUNT, inner_group).transpose(0, 2, 1, 3).reshape(N_DP, BUNDLE_SLOTCOUNT, HEADS * HEAD_DIM)

    def project(block_rows):
        return jnp.dot(block_rows, out_weight, preferred_element_type=jnp.float32).astype(jnp.bfloat16)
    return lax.map(project, normed)
```

```python
import jax
import jax.numpy as jnp
from jax import lax
from jax.sharding import PartitionSpec as P

BLOCK_LEN = 128


eps = 1e-05


def passed_along(block, axis, distance):
    devices = range(lax.axis_size(axis))
    route = [(i - distance, i) for i in devices if i - distance in devices]
    return lax.ppermute(block, axis, route)


def chain(gate, summed, axis):
    place = lax.axis_index(axis)

    def join(earlier, latter):
        return (earlier[0] * latter[0], latter[0][:, None, None] * earlier[1] + latter[1])

    def fetch(pair, distance):
        gate_in, summed_in = passed_along(
            (pair[0], pair[1].astype(jnp.bfloat16)), axis, distance
        )
        gate_in = jnp.where(place >= distance, gate_in, 1.0)
        return gate_in, summed_in.astype(jnp.float32)

    local = (gate, summed)
    before = fetch(local, 1)
    window = join(before, local)
    distance = 2
    while distance < lax.axis_size(axis):
        received = fetch(window, distance)
        before = join(received, before)
        distance *= 2
        if distance < lax.axis_size(axis):
            window = join(received, window)
    return before[1]


def conv_core(ext_values, weight, free_ext, length):
    tap_count = weight.shape[0]
    summed = jnp.zeros((length,) + ext_values.shape[1:], jnp.float32)
    keeping = jnp.ones((length,), jnp.float32)
    bshape = (length,) + (1,) * (ext_values.ndim - 1)
    for back in range(tap_count):
        if back > 0:
            keeping = keeping * free_ext[tap_count - back : tap_count - back + length]
        sample = ext_values[tap_count - 1 - back : tap_count - 1 - back + length].astype(
            jnp.float32
        )
        summed = summed + weight[tap_count - 1 - back] * sample * keeping.reshape(bshape)
    return jax.nn.silu(summed).astype(jnp.bfloat16)


def body(
    token_values,
    gate_values,
    state_maps,
    step_raw,
    log_rate,
    skip_gain,
    conv_values,
    conv_maps,
    piece_shift,
    doc_start,
    norm_gain,
    out_weight,
):
    owners = lax.axis_size(("dp", "ctx"))
    myself = lax.axis_index(("dp", "ctx"))
    slots = piece_shift.shape[0]
    rows = token_values.shape[1]
    piece_rows = rows // slots
    most = 2 * slots // owners
    slot_ids = jnp.arange(slots, dtype=jnp.int32)
    matching = piece_shift[:, None] == piece_shift[None, :]
    ranking = jnp.sum(
        (matching & (slot_ids[None, :] < slot_ids[:, None])).astype(jnp.int32), axis=1
    )
    offsets = (jnp.arange(owners, dtype=jnp.int32) - myself) % owners
    chosen = (piece_shift[None, None, :] == offsets[:, None, None]) & (
        ranking[None, None, :] == jnp.arange(most, dtype=jnp.int32)[None, :, None]
    )
    send_slot = jnp.sum(chosen.astype(jnp.int32) * slot_ids[None, None, :], axis=2)

    def outgoing(local):
        pieces = local[0].reshape((slots, piece_rows) + local.shape[2:])
        return pieces[send_slot]

    features = token_values.shape[2]
    map_shape = state_maps.shape[2:]
    map_width = map_shape[0] * map_shape[1]
    joined = jnp.concatenate(
        [token_values[0], state_maps[0].reshape(rows, map_width), step_raw[0]], axis=1
    )
    incoming = lax.all_to_all(
        outgoing(joined[None]), ("dp", "ctx"), split_axis=0, concat_axis=0, tiled=True
    )
    incoming_z = lax.all_to_all(
        outgoing(gate_values), ("dp", "ctx"), split_axis=0, concat_axis=0, tiled=True
    )
    source = (myself - piece_shift) % owners

    def placed(received):
        return received[source, ranking].reshape((rows,) + received.shape[3:])

    joined_pack = placed(incoming)
    z_pack = placed(incoming_z)
    margin = conv_values.shape[0] - 1
    flags = doc_start[0].astype(jnp.bfloat16)
    rim = passed_along(
        jnp.concatenate([joined_pack[rows - margin :], flags[rows - margin :, None]], axis=1),
        "ctx",
        1,
    )
    rim_x = rim[:, :features]
    rim_maps = rim[:, features : features + map_width].reshape((margin,) + map_shape)
    rim_flags = rim[:, -1]
    x_pack = joined_pack[:, :features]
    map_pack = joined_pack[:, features : features + map_width].reshape((rows,) + map_shape)
    dt_pack = joined_pack[:, features + map_width :]
    free_ext = 1.0 - jnp.concatenate([rim_flags, flags]).astype(jnp.float32)
    x_conv = conv_core(jnp.concatenate([rim_x, x_pack]), conv_values, free_ext, rows)
    map_conv = conv_core(jnp.concatenate([rim_maps, map_pack]), conv_maps, free_ext, rows)
    heads_local = log_rate.shape[0]
    groups_local = map_pack.shape[1]
    per_group = heads_local // groups_local
    width = x_pack.shape[1] // heads_local
    state = map_pack.shape[2] // 2
    span = BLOCK_LEN
    blocks = rows // span
    step_dt = jax.nn.softplus(dt_pack.astype(jnp.float32))
    log_decay = step_dt * (-jnp.exp(log_rate))[None, :]
    cum_t = jnp.cumsum(log_decay.reshape(blocks, span, heads_local), axis=1).transpose(0, 2, 1)
    dt_t = step_dt.reshape(blocks, span, heads_local).transpose(0, 2, 1)
    segment = jnp.cumsum(doc_start[0].reshape(blocks, span), axis=1)
    x_blocks = x_conv.reshape(blocks, span, groups_local, per_group, width)
    b_blocks = map_conv[:, :, :state].reshape(blocks, span, groups_local, state)
    c_blocks = map_conv[:, :, state:].reshape(blocks, span, groups_local, state)
    scores = jnp.einsum("bqgn,bsgn->bgqs", c_blocks, b_blocks, preferred_element_type=jnp.float32)
    later = jnp.arange(span)[:, None] >= jnp.arange(span)[None, :]
    allowed = later[None] & (segment[:, :, None] == segment[:, None, :])
    spread = cum_t[:, :, :, None] - cum_t[:, :, None, :]
    decay = jnp.exp(jnp.where(allowed[:, None], spread, -jnp.inf))
    weights = (
        decay.reshape(blocks, groups_local, per_group, span, span)
        * scores[:, :, None]
        * dt_t.reshape(blocks, groups_local, per_group, 1, span)
    ).astype(jnp.bfloat16)
    y_diag = jnp.einsum("bghts,bsghp->btghp", weights, x_blocks, preferred_element_type=jnp.float32)
    same_end = (segment == segment[:, -1:]).astype(jnp.float32)
    carry_coef = jnp.exp(cum_t[:, :, -1:] - cum_t) * dt_t * same_end[:, None, :]
    x_weighted = (
        x_blocks.astype(jnp.float32)
        * carry_coef.transpose(0, 2, 1).reshape(blocks, span, groups_local, per_group, 1)
    ).astype(jnp.bfloat16)
    block_states = jnp.einsum(
        "bsghp,bsgn->bghpn", x_weighted, b_blocks, preferred_element_type=jnp.float32
    ).reshape(blocks, heads_local, width, state)
    block_gates = jnp.exp(cum_t[:, :, -1]) * (segment[:, -1] == 0).astype(jnp.float32)[:, None]

    prior_states = [jnp.zeros_like(block_states[0])]
    prior_gates = [jnp.ones_like(block_gates[0])]
    for b in range(1, blocks):
        prior_states.append(block_gates[b - 1][:, None, None] * prior_states[-1] + block_states[b - 1])
        prior_gates.append(prior_gates[-1] * block_gates[b - 1])
    slab_state = block_gates[-1][:, None, None] * prior_states[-1] + block_states[-1]
    slab_gate = prior_gates[-1] * block_gates[-1]
    arriving = chain(slab_gate, slab_state, "ctx")
    entering = (
        (jnp.stack(prior_states) + jnp.stack(prior_gates)[:, :, None, None] * arriving[None])
        .astype(jnp.bfloat16)
        .reshape(blocks, groups_local, per_group, width, state)
    )
    y_off = jnp.einsum("bqgn,bghpn->bqghp", c_blocks, entering, preferred_element_type=jnp.float32)
    reach = (
        (jnp.exp(cum_t) * (segment == 0).astype(jnp.float32)[:, None, :])
        .transpose(0, 2, 1)
        .reshape(blocks, span, groups_local, per_group, 1)
    )
    mixed_y = (
        y_diag
        + y_off * reach
        + skip_gain.reshape(groups_local, per_group, 1) * x_blocks.astype(jnp.float32)
    )
    gated = mixed_y * jax.nn.silu(
        z_pack.astype(jnp.float32).reshape(blocks, span, groups_local, per_group, width)
    )
    power = jnp.mean(gated * gated, axis=(3, 4), keepdims=True)
    normed = (
        (gated * lax.rsqrt(power + eps) * norm_gain.reshape(groups_local, per_group, width))
        .astype(jnp.bfloat16)
        .reshape(rows, heads_local * width)
    )
    partial_value = jnp.dot(normed, out_weight, preferred_element_type=jnp.float32)
    result = lax.psum_scatter(
        partial_value.astype(jnp.bfloat16), "head", scatter_dimension=1, tiled=True
    )
    return result[None]


def solution(mesh):
    return jax.shard_map(
        body,
        mesh=mesh,
        in_specs=(
            P("dp", "ctx", "head"),
            P("dp", "ctx", "head"),
            P("dp", "ctx", "head", None),
            P("dp", "ctx", "head"),
            P("head"),
            P("head"),
            P(None, "head"),
            P(None, "head", None),
            P(),
            P("dp", "ctx"),
            P("head"),
            P("head", None),
        ),
        out_specs=P("dp", "ctx", "head"),
        check_vma=False,
    )
```

```python
import jax
import jax.numpy as jnp
from jax import lax
from jax.sharding import PartitionSpec as P

BLOCK_LEN = 128


eps = 1e-05


def passed_along(block, axis, distance):
    devices = range(lax.axis_size(axis))
    route = [(i - distance, i) for i in devices if i - distance in devices]
    return lax.ppermute(block, axis, route)


def chain(gate, summed, axis):
    place = lax.axis_index(axis)

    def join(earlier, latter):
        return (earlier[0] * latter[0], latter[0][:, None, None] * earlier[1] + latter[1])

    def fetch(pair, distance):
        gate_in, summed_in = passed_along(
            (pair[0], pair[1].astype(jnp.bfloat16)), axis, distance
        )
        gate_in = jnp.where(place >= distance, gate_in, 1.0)
        return gate_in, summed_in.astype(jnp.float32)

    local = (gate, summed)
    before = fetch(local, 1)
    window = join(before, local)
    distance = 2
    while distance < lax.axis_size(axis):
        received = fetch(window, distance)
        before = join(received, before)
        distance *= 2
        if distance < lax.axis_size(axis):
            window = join(received, window)
    return before[1]


def conv_core(ext_values, weight, free_ext, length):
    tap_count = weight.shape[0]
    summed = jnp.zeros((length,) + ext_values.shape[1:], jnp.float32)
    keeping = jnp.ones((length,), jnp.float32)
    bshape = (length,) + (1,) * (ext_values.ndim - 1)
    for back in range(tap_count):
        if back > 0:
            keeping = keeping * free_ext[tap_count - back : tap_count - back + length]
        sample = ext_values[tap_count - 1 - back : tap_count - 1 - back + length].astype(
            jnp.float32
        )
        summed = summed + weight[tap_count - 1 - back] * sample * keeping.reshape(bshape)
    return jax.nn.silu(summed).astype(jnp.bfloat16)


def body(
    token_values,
    gate_values,
    state_maps,
    step_raw,
    log_rate,
    skip_gain,
    conv_values,
    conv_maps,
    piece_shift,
    doc_start,
    norm_gain,
    out_weight,
):
    owners = lax.axis_size(("dp", "ctx"))
    myself = lax.axis_index(("dp", "ctx"))
    slots = piece_shift.shape[0]
    rows = token_values.shape[1]
    piece_rows = rows // slots
    slot_ids = jnp.arange(slots, dtype=jnp.int32)
    matching = piece_shift[:, None] == piece_shift[None, :]
    ranking = jnp.sum(
        (matching & (slot_ids[None, :] < slot_ids[:, None])).astype(jnp.int32), axis=1
    )
    leading = ranking == 0
    offsets = (jnp.arange(owners, dtype=jnp.int32) - myself) % owners
    holds = (piece_shift[None, :] == jnp.arange(owners, dtype=jnp.int32)[:, None]) & leading
    first_of = jnp.argmax(holds, axis=1).astype(jnp.int32)
    send_slot = first_of[offsets]
    source = (myself - piece_shift) % owners
    trailing = jnp.logical_not(leading)
    extra_count = jnp.sum(trailing.astype(jnp.int32))
    extra_order = jnp.argsort(jnp.where(trailing, slot_ids, slots + slot_ids)).astype(jnp.int32)

    features = token_values.shape[2]
    map_shape = state_maps.shape[2:]
    map_width = map_shape[0] * map_shape[1]
    joined = jnp.concatenate(
        [token_values[0], state_maps[0].reshape(rows, map_width), step_raw[0]], axis=1
    ).reshape(slots, piece_rows, -1)
    gates_local = gate_values[0].reshape(slots, piece_rows, -1)

    def routed_first(pieces):
        received = lax.all_to_all(
            pieces[send_slot], ("dp", "ctx"), split_axis=0, concat_axis=0, tiled=True
        )
        return received[source]

    def shifter(distance):
        if distance == 0:
            return lambda pair: pair
        route = [(i, (i + distance) % owners) for i in range(owners)]
        return lambda pair: lax.ppermute(pair, ("dp", "ctx"), route)

    branches = [shifter(distance) for distance in range(owners)]

    def one_extra(i, bufs):
        slot = extra_order[i]
        pair = (
            lax.dynamic_index_in_dim(joined, slot, 0, False),
            lax.dynamic_index_in_dim(gates_local, slot, 0, False),
        )
        got = lax.switch(piece_shift[slot], branches, pair)
        return tuple(
            lax.dynamic_update_index_in_dim(buf, part, slot, 0) for buf, part in zip(bufs, got)
        )

    extra_joined, extra_gates = lax.fori_loop(
        0, extra_count, one_extra, (jnp.zeros_like(joined), jnp.zeros_like(gates_local))
    )
    keep_first = leading[:, None, None]
    joined_pack = jnp.where(keep_first, routed_first(joined), extra_joined).reshape(rows, -1)
    z_pack = jnp.where(keep_first, routed_first(gates_local), extra_gates).reshape(rows, -1)
    margin = conv_values.shape[0] - 1
    flags = doc_start[0].astype(jnp.bfloat16)
    rim = passed_along(
        jnp.concatenate([joined_pack[rows - margin :], flags[rows - margin :, None]], axis=1),
        "ctx",
        1,
    )
    rim_x = rim[:, :features]
    rim_maps = rim[:, features : features + map_width].reshape((margin,) + map_shape)
    rim_flags = rim[:, -1]
    x_pack = joined_pack[:, :features]
    map_pack = joined_pack[:, features : features + map_width].reshape((rows,) + map_shape)
    dt_pack = joined_pack[:, features + map_width :]
    free_ext = 1.0 - jnp.concatenate([rim_flags, flags]).astype(jnp.float32)
    x_conv = conv_core(jnp.concatenate([rim_x, x_pack]), conv_values, free_ext, rows)
    map_conv = conv_core(jnp.concatenate([rim_maps, map_pack]), conv_maps, free_ext, rows)
    heads_local = log_rate.shape[0]
    groups_local = map_pack.shape[1]
    per_group = heads_local // groups_local
    width = x_pack.shape[1] // heads_local
    state = map_pack.shape[2] // 2
    span = BLOCK_LEN
    blocks = rows // span
    step_dt = jax.nn.softplus(dt_pack.astype(jnp.float32))
    log_decay = step_dt * (-jnp.exp(log_rate))[None, :]
    cum_t = jnp.cumsum(log_decay.reshape(blocks, span, heads_local), axis=1).transpose(0, 2, 1)
    dt_t = step_dt.reshape(blocks, span, heads_local).transpose(0, 2, 1)
    segment = jnp.cumsum(doc_start[0].reshape(blocks, span), axis=1)
    x_blocks = x_conv.reshape(blocks, span, groups_local, per_group, width)
    b_blocks = map_conv[:, :, :state].reshape(blocks, span, groups_local, state)
    c_blocks = map_conv[:, :, state:].reshape(blocks, span, groups_local, state)
    scores = jnp.einsum("bqgn,bsgn->bgqs", c_blocks, b_blocks, preferred_element_type=jnp.float32)
    later = jnp.arange(span)[:, None] >= jnp.arange(span)[None, :]
    allowed = later[None] & (segment[:, :, None] == segment[:, None, :])
    spread = cum_t[:, :, :, None] - cum_t[:, :, None, :]
    decay = jnp.exp(jnp.where(allowed[:, None], spread, -jnp.inf))
    weights = (
        decay.reshape(blocks, groups_local, per_group, span, span)
        * scores[:, :, None]
        * dt_t.reshape(blocks, groups_local, per_group, 1, span)
    ).astype(jnp.bfloat16)
    y_diag = jnp.einsum("bghts,bsghp->btghp", weights, x_blocks, preferred_element_type=jnp.float32)
    same_end = (segment == segment[:, -1:]).astype(jnp.float32)
    carry_coef = jnp.exp(cum_t[:, :, -1:] - cum_t) * dt_t * same_end[:, None, :]
    x_weighted = (
        x_blocks.astype(jnp.float32)
        * carry_coef.transpose(0, 2, 1).reshape(blocks, span, groups_local, per_group, 1)
    ).astype(jnp.bfloat16)
    block_states = jnp.einsum(
        "bsghp,bsgn->bghpn", x_weighted, b_blocks, preferred_element_type=jnp.float32
    ).reshape(blocks, heads_local, width, state)
    block_gates = jnp.exp(cum_t[:, :, -1]) * (segment[:, -1] == 0).astype(jnp.float32)[:, None]

    prior_states = [jnp.zeros_like(block_states[0])]
    prior_gates = [jnp.ones_like(block_gates[0])]
    for b in range(1, blocks):
        prior_states.append(block_gates[b - 1][:, None, None] * prior_states[-1] + block_states[b - 1])
        prior_gates.append(prior_gates[-1] * block_gates[b - 1])
    slab_state = block_gates[-1][:, None, None] * prior_states[-1] + block_states[-1]
    slab_gate = prior_gates[-1] * block_gates[-1]
    arriving = chain(slab_gate, slab_state, "ctx")
    entering = (
        (jnp.stack(prior_states) + jnp.stack(prior_gates)[:, :, None, None] * arriving[None])
        .astype(jnp.bfloat16)
        .reshape(blocks, groups_local, per_group, width, state)
    )
    reach = (
        (jnp.exp(cum_t) * (segment == 0).astype(jnp.float32)[:, None, :])
        .transpose(0, 2, 1)
        .reshape(blocks, span, groups_local, per_group, 1)
    )
    skip_rows = skip_gain.reshape(groups_local, per_group, 1)
    gain_rows = norm_gain.reshape(groups_local, per_group, width)
    pieces_out = []
    for b in range(blocks):
        y_off = jnp.einsum(
            "qgn,ghpn->qghp", c_blocks[b], entering[b], preferred_element_type=jnp.float32
        )
        mixed_y = y_diag[b] + y_off * reach[b] + skip_rows * x_blocks[b].astype(jnp.float32)
        gated = mixed_y * jax.nn.silu(
            z_pack[b * span : (b + 1) * span]
            .astype(jnp.float32)
            .reshape(span, groups_local, per_group, width)
        )
        power = jnp.mean(gated * gated, axis=(2, 3), keepdims=True)
        normed = (
            (gated * lax.rsqrt(power + eps) * gain_rows)
            .astype(jnp.bfloat16)
            .reshape(span, heads_local * width)
        )
        partial_value = jnp.dot(normed, out_weight, preferred_element_type=jnp.float32)
        pieces_out.append(
            lax.psum_scatter(
                partial_value.astype(jnp.bfloat16), "head", scatter_dimension=1, tiled=True
            )
        )
    result = jnp.concatenate(pieces_out, axis=0)
    return result[None]


def solution(mesh):
    return jax.shard_map(
        body,
        mesh=mesh,
        in_specs=(
            P("dp", "ctx", "head"),
            P("dp", "ctx", "head"),
            P("dp", "ctx", "head", None),
            P("dp", "ctx", "head"),
            P("head"),
            P("head"),
            P(None, "head"),
            P(None, "head", None),
            P(),
            P("dp", "ctx"),
            P("head"),
            P("head", None),
        ),
        out_specs=P("dp", "ctx", "head"),
        check_vma=False,
    )
```

```python
import jax
import jax.numpy as jnp
from jax import lax
from jax.sharding import PartitionSpec as P

BLOCK_LEN = 128


eps = 1e-05


def passed_along(block, axis, distance):
    devices = range(lax.axis_size(axis))
    route = [(i - distance, i) for i in devices if i - distance in devices]
    return lax.ppermute(block, axis, route)


def chain(gate, summed, axis):
    place = lax.axis_index(axis)

    def join(earlier, latter):
        return (earlier[0] * latter[0], latter[0][:, None, None] * earlier[1] + latter[1])

    def fetch(pair, distance):
        gate_in, summed_in = passed_along(
            (pair[0], pair[1].astype(jnp.bfloat16)), axis, distance
        )
        gate_in = jnp.where(place >= distance, gate_in, 1.0)
        return gate_in, summed_in.astype(jnp.float32)

    local = (gate, summed)
    before = fetch(local, 1)
    window = join(before, local)
    distance = 2
    while distance < lax.axis_size(axis):
        received = fetch(window, distance)
        before = join(received, before)
        distance *= 2
        if distance < lax.axis_size(axis):
            window = join(received, window)
    return before[1]


def conv_core(ext_values, weight, free_ext, length):
    tap_count = weight.shape[0]
    summed = jnp.zeros((length,) + ext_values.shape[1:], jnp.float32)
    keeping = jnp.ones((length,), jnp.float32)
    bshape = (length,) + (1,) * (ext_values.ndim - 1)
    for back in range(tap_count):
        if back > 0:
            keeping = keeping * free_ext[tap_count - back : tap_count - back + length]
        sample = ext_values[tap_count - 1 - back : tap_count - 1 - back + length].astype(
            jnp.float32
        )
        summed = summed + weight[tap_count - 1 - back] * sample * keeping.reshape(bshape)
    return jax.nn.silu(summed).astype(jnp.bfloat16)


def body(
    token_values,
    gate_values,
    state_maps,
    step_raw,
    log_rate,
    skip_gain,
    conv_values,
    conv_maps,
    piece_shift,
    doc_start,
    norm_gain,
    out_weight,
):
    owners = lax.axis_size(("dp", "ctx"))
    myself = lax.axis_index(("dp", "ctx"))
    slots = piece_shift.shape[0]
    rows = token_values.shape[1]
    piece_rows = rows // slots
    most = 2 * slots // owners
    slot_ids = jnp.arange(slots, dtype=jnp.int32)
    matching = piece_shift[:, None] == piece_shift[None, :]
    ranking = jnp.sum(
        (matching & (slot_ids[None, :] < slot_ids[:, None])).astype(jnp.int32), axis=1
    )
    offsets = (jnp.arange(owners, dtype=jnp.int32) - myself) % owners
    chosen = (piece_shift[None, None, :] == jnp.arange(owners, dtype=jnp.int32)[:, None, None]) & (
        ranking[None, None, :] == jnp.arange(most, dtype=jnp.int32)[None, :, None]
    )
    slot_of = jnp.sum(chosen.astype(jnp.int32) * slot_ids[None, None, :], axis=2)
    send_slots = [slot_of[offsets, rank] for rank in range(most)]
    source = (myself - piece_shift) % owners

    def routed(local):
        pieces = local.reshape((slots, piece_rows) + local.shape[1:])
        result = None
        for rank in range(most):
            received = lax.all_to_all(
                pieces[send_slots[rank]], ("dp", "ctx"), split_axis=0, concat_axis=0, tiled=True
            )[source]
            if result is None:
                result = received
            else:
                result = jnp.where((ranking == rank)[:, None, None], received, result)
        return result.reshape((rows,) + local.shape[1:])

    features = token_values.shape[2]
    map_shape = state_maps.shape[2:]
    map_width = map_shape[0] * map_shape[1]
    joined = jnp.concatenate(
        [token_values[0], state_maps[0].reshape(rows, map_width), step_raw[0]], axis=1
    )
    joined_pack = routed(joined)
    z_pack = routed(gate_values[0])
    margin = conv_values.shape[0] - 1
    flags = doc_start[0].astype(jnp.bfloat16)
    rim = passed_along(
        jnp.concatenate([joined_pack[rows - margin :], flags[rows - margin :, None]], axis=1),
        "ctx",
        1,
    )
    rim_x = rim[:, :features]
    rim_maps = rim[:, features : features + map_width].reshape((margin,) + map_shape)
    rim_flags = rim[:, -1]
    x_pack = joined_pack[:, :features]
    map_pack = joined_pack[:, features : features + map_width].reshape((rows,) + map_shape)
    dt_pack = joined_pack[:, features + map_width :]
    free_ext = 1.0 - jnp.concatenate([rim_flags, flags]).astype(jnp.float32)
    x_conv = conv_core(jnp.concatenate([rim_x, x_pack]), conv_values, free_ext, rows)
    map_conv = conv_core(jnp.concatenate([rim_maps, map_pack]), conv_maps, free_ext, rows)
    heads_local = log_rate.shape[0]
    groups_local = map_pack.shape[1]
    per_group = heads_local // groups_local
    width = x_pack.shape[1] // heads_local
    state = map_pack.shape[2] // 2
    span = BLOCK_LEN
    blocks = rows // span
    step_dt = jax.nn.softplus(dt_pack.astype(jnp.float32))
    log_decay = step_dt * (-jnp.exp(log_rate))[None, :]
    cum_t = jnp.cumsum(log_decay.reshape(blocks, span, heads_local), axis=1).transpose(0, 2, 1)
    dt_t = step_dt.reshape(blocks, span, heads_local).transpose(0, 2, 1)
    segment = jnp.cumsum(doc_start[0].reshape(blocks, span), axis=1)
    x_blocks = x_conv.reshape(blocks, span, groups_local, per_group, width)
    b_blocks = map_conv[:, :, :state].reshape(blocks, span, groups_local, state)
    c_blocks = map_conv[:, :, state:].reshape(blocks, span, groups_local, state)
    scores = jnp.einsum("bqgn,bsgn->bgqs", c_blocks, b_blocks, preferred_element_type=jnp.float32)
    later = jnp.arange(span)[:, None] >= jnp.arange(span)[None, :]
    allowed = later[None] & (segment[:, :, None] == segment[:, None, :])
    spread = cum_t[:, :, :, None] - cum_t[:, :, None, :]
    decay = jnp.exp(jnp.where(allowed[:, None], spread, -jnp.inf))
    weights = (
        decay.reshape(blocks, groups_local, per_group, span, span)
        * scores[:, :, None]
        * dt_t.reshape(blocks, groups_local, per_group, 1, span)
    ).astype(jnp.bfloat16)
    y_diag = jnp.einsum("bghts,bsghp->btghp", weights, x_blocks, preferred_element_type=jnp.float32)
    same_end = (segment == segment[:, -1:]).astype(jnp.float32)
    carry_coef = jnp.exp(cum_t[:, :, -1:] - cum_t) * dt_t * same_end[:, None, :]
    x_weighted = (
        x_blocks.astype(jnp.float32)
        * carry_coef.transpose(0, 2, 1).reshape(blocks, span, groups_local, per_group, 1)
    ).astype(jnp.bfloat16)
    block_states = jnp.einsum(
        "bsghp,bsgn->bghpn", x_weighted, b_blocks, preferred_element_type=jnp.float32
    ).reshape(blocks, heads_local, width, state)
    block_gates = jnp.exp(cum_t[:, :, -1]) * (segment[:, -1] == 0).astype(jnp.float32)[:, None]

    prior_states = [jnp.zeros_like(block_states[0])]
    prior_gates = [jnp.ones_like(block_gates[0])]
    for b in range(1, blocks):
        prior_states.append(block_gates[b - 1][:, None, None] * prior_states[-1] + block_states[b - 1])
        prior_gates.append(prior_gates[-1] * block_gates[b - 1])
    slab_state = block_gates[-1][:, None, None] * prior_states[-1] + block_states[-1]
    slab_gate = prior_gates[-1] * block_gates[-1]
    arriving = chain(slab_gate, slab_state, "ctx")
    entering = (
        (jnp.stack(prior_states) + jnp.stack(prior_gates)[:, :, None, None] * arriving[None])
        .astype(jnp.bfloat16)
        .reshape(blocks, groups_local, per_group, width, state)
    )
    y_off = jnp.einsum("bqgn,bghpn->bqghp", c_blocks, entering, preferred_element_type=jnp.float32)
    reach = (
        (jnp.exp(cum_t) * (segment == 0).astype(jnp.float32)[:, None, :])
        .transpose(0, 2, 1)
        .reshape(blocks, span, groups_local, per_group, 1)
    )
    mixed_y = (
        y_diag
        + y_off * reach
        + skip_gain.reshape(groups_local, per_group, 1) * x_blocks.astype(jnp.float32)
    )
    gated = mixed_y * jax.nn.silu(
        z_pack.astype(jnp.float32).reshape(blocks, span, groups_local, per_group, width)
    )
    power = jnp.mean(gated * gated, axis=(3, 4), keepdims=True)
    normed = (
        (gated * lax.rsqrt(power + eps) * norm_gain.reshape(groups_local, per_group, width))
        .astype(jnp.bfloat16)
        .reshape(rows, heads_local * width)
    )
    partial_value = jnp.dot(normed, out_weight, preferred_element_type=jnp.float32)
    result = lax.psum_scatter(
        partial_value.astype(jnp.bfloat16), "head", scatter_dimension=1, tiled=True
    )
    return result[None]


def solution(mesh):
    return jax.shard_map(
        body,
        mesh=mesh,
        in_specs=(
            P("dp", "ctx", "head"),
            P("dp", "ctx", "head"),
            P("dp", "ctx", "head", None),
            P("dp", "ctx", "head"),
            P("head"),
            P("head"),
            P(None, "head"),
            P(None, "head", None),
            P(),
            P("dp", "ctx"),
            P("head"),
            P("head", None),
        ),
        out_specs=P("dp", "ctx", "head"),
        check_vma=False,
    )
```

```python
import jax
import jax.numpy as jnp
from jax import lax
from jax.sharding import PartitionSpec as P

BLOCK_LEN = 128


eps = 1e-05


def passed_along(block, axis, distance):
    devices = range(lax.axis_size(axis))
    route = [(i - distance, i) for i in devices if i - distance in devices]
    return lax.ppermute(block, axis, route)


def chain(gate, summed, axis):
    place = lax.axis_index(axis)

    def join(earlier, latter):
        return (earlier[0] * latter[0], latter[0][:, None, None] * earlier[1] + latter[1])

    def fetch(pair, distance):
        gate_in, summed_in = passed_along(
            (pair[0], pair[1].astype(jnp.bfloat16)), axis, distance
        )
        gate_in = jnp.where(place >= distance, gate_in, 1.0)
        return gate_in, summed_in.astype(jnp.float32)

    local = (gate, summed)
    before = fetch(local, 1)
    window = join(before, local)
    distance = 2
    while distance < lax.axis_size(axis):
        received = fetch(window, distance)
        before = join(received, before)
        distance *= 2
        if distance < lax.axis_size(axis):
            window = join(received, window)
    return before[1]


def ring_scatter(partial_value, axis):
    count = lax.axis_size(axis)
    place = lax.axis_index(axis)
    rows, total = partial_value.shape
    half = rows // 2
    by_block = partial_value.reshape(rows, count, total // count)

    def block(lo, index):
        return lax.dynamic_index_in_dim(by_block[lo : lo + half], index % count, 1, False)

    upward = [(i, (i + 1) % count) for i in range(count)]
    downward = [(i, (i - 1) % count) for i in range(count)]
    rising = block(0, place - 1)
    falling = block(half, place + 1)
    for step in range(1, count):
        rising = lax.ppermute(rising.astype(jnp.bfloat16), axis, upward)
        falling = lax.ppermute(falling.astype(jnp.bfloat16), axis, downward)
        rising = rising.astype(jnp.float32) + block(0, place - step - 1)
        falling = falling.astype(jnp.float32) + block(half, place + step + 1)
    return jnp.concatenate([rising, falling], axis=0).astype(jnp.bfloat16)


def conv_core(ext_values, weight, free_ext, length):
    tap_count = weight.shape[0]
    summed = jnp.zeros((length,) + ext_values.shape[1:], jnp.float32)
    keeping = jnp.ones((length,), jnp.float32)
    bshape = (length,) + (1,) * (ext_values.ndim - 1)
    for back in range(tap_count):
        if back > 0:
            keeping = keeping * free_ext[tap_count - back : tap_count - back + length]
        sample = ext_values[tap_count - 1 - back : tap_count - 1 - back + length].astype(
            jnp.float32
        )
        summed = summed + weight[tap_count - 1 - back] * sample * keeping.reshape(bshape)
    return jax.nn.silu(summed).astype(jnp.bfloat16)


def body(
    token_values,
    gate_values,
    state_maps,
    step_raw,
    log_rate,
    skip_gain,
    conv_values,
    conv_maps,
    piece_shift,
    doc_start,
    norm_gain,
    out_weight,
):
    owners = lax.axis_size(("dp", "ctx"))
    myself = lax.axis_index(("dp", "ctx"))
    slots = piece_shift.shape[0]
    rows = token_values.shape[1]
    piece_rows = rows // slots
    most = 2 * slots // owners
    slot_ids = jnp.arange(slots, dtype=jnp.int32)
    matching = piece_shift[:, None] == piece_shift[None, :]
    ranking = jnp.sum(
        (matching & (slot_ids[None, :] < slot_ids[:, None])).astype(jnp.int32), axis=1
    )
    offsets = (jnp.arange(owners, dtype=jnp.int32) - myself) % owners
    chosen = (piece_shift[None, None, :] == offsets[:, None, None]) & (
        ranking[None, None, :] == jnp.arange(most, dtype=jnp.int32)[None, :, None]
    )
    send_slot = jnp.sum(chosen.astype(jnp.int32) * slot_ids[None, None, :], axis=2)

    def outgoing(local):
        pieces = local[0].reshape((slots, piece_rows) + local.shape[2:])
        return pieces[send_slot]

    features = token_values.shape[2]
    map_shape = state_maps.shape[2:]
    map_width = map_shape[0] * map_shape[1]
    joined = jnp.concatenate(
        [token_values[0], state_maps[0].reshape(rows, map_width), step_raw[0]], axis=1
    )
    incoming = lax.all_to_all(
        outgoing(joined[None]), ("dp", "ctx"), split_axis=0, concat_axis=0, tiled=True
    )
    incoming_z = lax.all_to_all(
        outgoing(gate_values), ("dp", "ctx"), split_axis=0, concat_axis=0, tiled=True
    )
    source = (myself - piece_shift) % owners

    def placed(received):
        return received[source, ranking].reshape((rows,) + received.shape[3:])

    joined_pack = placed(incoming)
    z_pack = placed(incoming_z)
    margin = conv_values.shape[0] - 1
    flags = doc_start[0].astype(jnp.bfloat16)
    rim = passed_along(
        jnp.concatenate([joined_pack[rows - margin :], flags[rows - margin :, None]], axis=1),
        "ctx",
        1,
    )
    rim_x = rim[:, :features]
    rim_maps = rim[:, features : features + map_width].reshape((margin,) + map_shape)
    rim_flags = rim[:, -1]
    x_pack = joined_pack[:, :features]
    map_pack = joined_pack[:, features : features + map_width].reshape((rows,) + map_shape)
    dt_pack = joined_pack[:, features + map_width :]
    free_ext = 1.0 - jnp.concatenate([rim_flags, flags]).astype(jnp.float32)
    x_conv = conv_core(jnp.concatenate([rim_x, x_pack]), conv_values, free_ext, rows)
    map_conv = conv_core(jnp.concatenate([rim_maps, map_pack]), conv_maps, free_ext, rows)
    heads_local = log_rate.shape[0]
    groups_local = map_pack.shape[1]
    per_group = heads_local // groups_local
    width = x_pack.shape[1] // heads_local
    state = map_pack.shape[2] // 2
    span = BLOCK_LEN
    blocks = rows // span
    step_dt = jax.nn.softplus(dt_pack.astype(jnp.float32))
    log_decay = step_dt * (-jnp.exp(log_rate))[None, :]
    cum_t = jnp.cumsum(log_decay.reshape(blocks, span, heads_local), axis=1).transpose(0, 2, 1)
    dt_t = step_dt.reshape(blocks, span, heads_local).transpose(0, 2, 1)
    segment = jnp.cumsum(doc_start[0].reshape(blocks, span), axis=1)
    x_blocks = x_conv.reshape(blocks, span, groups_local, per_group, width)
    b_blocks = map_conv[:, :, :state].reshape(blocks, span, groups_local, state)
    c_blocks = map_conv[:, :, state:].reshape(blocks, span, groups_local, state)
    scores = jnp.einsum("bqgn,bsgn->bgqs", c_blocks, b_blocks, preferred_element_type=jnp.float32)
    later = jnp.arange(span)[:, None] >= jnp.arange(span)[None, :]
    allowed = later[None] & (segment[:, :, None] == segment[:, None, :])
    spread = cum_t[:, :, :, None] - cum_t[:, :, None, :]
    decay = jnp.exp(jnp.where(allowed[:, None], spread, -jnp.inf))
    weights = (
        decay.reshape(blocks, groups_local, per_group, span, span)
        * scores[:, :, None]
        * dt_t.reshape(blocks, groups_local, per_group, 1, span)
    ).astype(jnp.bfloat16)
    y_diag = jnp.einsum("bghts,bsghp->btghp", weights, x_blocks, preferred_element_type=jnp.float32)
    same_end = (segment == segment[:, -1:]).astype(jnp.float32)
    carry_coef = jnp.exp(cum_t[:, :, -1:] - cum_t) * dt_t * same_end[:, None, :]
    x_weighted = (
        x_blocks.astype(jnp.float32)
        * carry_coef.transpose(0, 2, 1).reshape(blocks, span, groups_local, per_group, 1)
    ).astype(jnp.bfloat16)
    block_states = jnp.einsum(
        "bsghp,bsgn->bghpn", x_weighted, b_blocks, preferred_element_type=jnp.float32
    ).reshape(blocks, heads_local, width, state)
    block_gates = jnp.exp(cum_t[:, :, -1]) * (segment[:, -1] == 0).astype(jnp.float32)[:, None]

    prior_states = [jnp.zeros_like(block_states[0])]
    prior_gates = [jnp.ones_like(block_gates[0])]
    for b in range(1, blocks):
        prior_states.append(block_gates[b - 1][:, None, None] * prior_states[-1] + block_states[b - 1])
        prior_gates.append(prior_gates[-1] * block_gates[b - 1])
    slab_state = block_gates[-1][:, None, None] * prior_states[-1] + block_states[-1]
    slab_gate = prior_gates[-1] * block_gates[-1]
    arriving = chain(slab_gate, slab_state, "ctx")
    entering = (
        (jnp.stack(prior_states) + jnp.stack(prior_gates)[:, :, None, None] * arriving[None])
        .astype(jnp.bfloat16)
        .reshape(blocks, groups_local, per_group, width, state)
    )
    y_off = jnp.einsum("bqgn,bghpn->bqghp", c_blocks, entering, preferred_element_type=jnp.float32)
    reach = (
        (jnp.exp(cum_t) * (segment == 0).astype(jnp.float32)[:, None, :])
        .transpose(0, 2, 1)
        .reshape(blocks, span, groups_local, per_group, 1)
    )
    mixed_y = (
        y_diag
        + y_off * reach
        + skip_gain.reshape(groups_local, per_group, 1) * x_blocks.astype(jnp.float32)
    )
    gated = mixed_y * jax.nn.silu(
        z_pack.astype(jnp.float32).reshape(blocks, span, groups_local, per_group, width)
    )
    power = jnp.mean(gated * gated, axis=(3, 4), keepdims=True)
    normed = (
        (gated * lax.rsqrt(power + eps) * norm_gain.reshape(groups_local, per_group, width))
        .astype(jnp.bfloat16)
        .reshape(rows, heads_local * width)
    )
    partial_value = jnp.dot(normed, out_weight, preferred_element_type=jnp.float32)
    result = ring_scatter(partial_value, "head")
    return result[None]


def solution(mesh):
    return jax.shard_map(
        body,
        mesh=mesh,
        in_specs=(
            P("dp", "ctx", "head"),
            P("dp", "ctx", "head"),
            P("dp", "ctx", "head", None),
            P("dp", "ctx", "head"),
            P("head"),
            P("head"),
            P(None, "head"),
            P(None, "head", None),
            P(),
            P("dp", "ctx"),
            P("head"),
            P("head", None),
        ),
        out_specs=P("dp", "ctx", "head"),
        check_vma=False,
    )
```

```python
import jax
import jax.numpy as jnp
from jax import lax
from jax.sharding import PartitionSpec as P

BLOCK_LEN = 128


eps = 1e-05


def passed_along(block, axis, distance):
    devices = range(lax.axis_size(axis))
    route = [(i - distance, i) for i in devices if i - distance in devices]
    return lax.ppermute(block, axis, route)


def chain(gate, summed, axis):
    place = lax.axis_index(axis)

    def join(earlier, latter):
        return (earlier[0] * latter[0], latter[0][:, None, None] * earlier[1] + latter[1])

    def fetch(pair, distance):
        gate_in, summed_in = passed_along(
            (pair[0], pair[1].astype(jnp.bfloat16)), axis, distance
        )
        gate_in = jnp.where(place >= distance, gate_in, 1.0)
        return gate_in, summed_in.astype(jnp.float32)

    local = (gate, summed)
    before = fetch(local, 1)
    window = join(before, local)
    distance = 2
    while distance < lax.axis_size(axis):
        received = fetch(window, distance)
        before = join(received, before)
        distance *= 2
        if distance < lax.axis_size(axis):
            window = join(received, window)
    return before[1]


def conv_core(ext_values, weight, free_ext, length):
    tap_count = weight.shape[0]
    summed = jnp.zeros((length,) + ext_values.shape[1:], jnp.float32)
    keeping = jnp.ones((length,), jnp.float32)
    bshape = (length,) + (1,) * (ext_values.ndim - 1)
    for back in range(tap_count):
        if back > 0:
            keeping = keeping * free_ext[tap_count - back : tap_count - back + length]
        sample = ext_values[tap_count - 1 - back : tap_count - 1 - back + length].astype(
            jnp.float32
        )
        summed = summed + weight[tap_count - 1 - back] * sample * keeping.reshape(bshape)
    return jax.nn.silu(summed).astype(jnp.bfloat16)


def body(
    token_values,
    gate_values,
    state_maps,
    step_raw,
    log_rate,
    skip_gain,
    conv_values,
    conv_maps,
    piece_shift,
    doc_start,
    norm_gain,
    out_weight,
):
    owners = lax.axis_size(("dp", "ctx"))
    myself = lax.axis_index(("dp", "ctx"))
    slots = piece_shift.shape[0]
    rows = token_values.shape[1]
    piece_rows = rows // slots
    most = 2 * slots // owners
    slot_ids = jnp.arange(slots, dtype=jnp.int32)
    matching = piece_shift[:, None] == piece_shift[None, :]
    ranking = jnp.sum(
        (matching & (slot_ids[None, :] < slot_ids[:, None])).astype(jnp.int32), axis=1
    )
    offsets = (jnp.arange(owners, dtype=jnp.int32) - myself) % owners
    chosen = (piece_shift[None, None, :] == offsets[:, None, None]) & (
        ranking[None, None, :] == jnp.arange(most, dtype=jnp.int32)[None, :, None]
    )
    send_slot = jnp.sum(chosen.astype(jnp.int32) * slot_ids[None, None, :], axis=2)

    def outgoing(local):
        pieces = local[0].reshape((slots, piece_rows) + local.shape[2:])
        return pieces[send_slot]

    features = token_values.shape[2]
    map_shape = state_maps.shape[2:]
    map_width = map_shape[0] * map_shape[1]
    joined = jnp.concatenate(
        [token_values[0], state_maps[0].reshape(rows, map_width), step_raw[0]], axis=1
    )
    incoming = lax.all_to_all(
        outgoing(joined[None]), ("dp", "ctx"), split_axis=0, concat_axis=0, tiled=True
    )
    incoming_z = lax.all_to_all(
        outgoing(gate_values), ("dp", "ctx"), split_axis=0, concat_axis=0, tiled=True
    )
    source = (myself - piece_shift) % owners

    def placed(received):
        return received[source, ranking].reshape((rows,) + received.shape[3:])

    joined_pack = placed(incoming)
    margin = conv_values.shape[0] - 1
    flags = doc_start[0].astype(jnp.bfloat16)
    rim = passed_along(
        jnp.concatenate([joined_pack[rows - margin :], flags[rows - margin :, None]], axis=1),
        "ctx",
        1,
    )
    rim_x = rim[:, :features]
    rim_maps = rim[:, features : features + map_width].reshape((margin,) + map_shape)
    rim_flags = rim[:, -1]
    x_pack = joined_pack[:, :features]
    map_pack = joined_pack[:, features : features + map_width].reshape((rows,) + map_shape)
    dt_pack = joined_pack[:, features + map_width :]
    free_ext = 1.0 - jnp.concatenate([rim_flags, flags]).astype(jnp.float32)
    x_conv = conv_core(jnp.concatenate([rim_x, x_pack]), conv_values, free_ext, rows)
    map_conv = conv_core(jnp.concatenate([rim_maps, map_pack]), conv_maps, free_ext, rows)
    heads_local = log_rate.shape[0]
    groups_local = map_pack.shape[1]
    per_group = heads_local // groups_local
    width = x_pack.shape[1] // heads_local
    state = map_pack.shape[2] // 2
    span = BLOCK_LEN
    blocks = rows // span
    step_dt = jax.nn.softplus(dt_pack.astype(jnp.float32))
    log_decay = step_dt * (-jnp.exp(log_rate))[None, :]
    cum_t = jnp.cumsum(log_decay.reshape(blocks, span, heads_local), axis=1).transpose(0, 2, 1)
    dt_t = step_dt.reshape(blocks, span, heads_local).transpose(0, 2, 1)
    segment = jnp.cumsum(doc_start[0].reshape(blocks, span), axis=1)
    x_blocks = x_conv.reshape(blocks, span, groups_local, per_group, width)
    b_blocks = map_conv[:, :, :state].reshape(blocks, span, groups_local, state)
    c_blocks = map_conv[:, :, state:].reshape(blocks, span, groups_local, state)
    scores = jnp.einsum("bqgn,bsgn->bgqs", c_blocks, b_blocks, preferred_element_type=jnp.float32)
    later = jnp.arange(span)[:, None] >= jnp.arange(span)[None, :]
    allowed = later[None] & (segment[:, :, None] == segment[:, None, :])
    spread = cum_t[:, :, :, None] - cum_t[:, :, None, :]
    decay = jnp.exp(jnp.where(allowed[:, None], spread, -jnp.inf))
    weights = (
        decay.reshape(blocks, groups_local, per_group, span, span)
        * scores[:, :, None]
        * dt_t.reshape(blocks, groups_local, per_group, 1, span)
    ).astype(jnp.bfloat16)
    y_diag = jnp.einsum("bghts,bsghp->btghp", weights, x_blocks, preferred_element_type=jnp.float32)
    same_end = (segment == segment[:, -1:]).astype(jnp.float32)
    carry_coef = jnp.exp(cum_t[:, :, -1:] - cum_t) * dt_t * same_end[:, None, :]
    x_weighted = (
        x_blocks.astype(jnp.float32)
        * carry_coef.transpose(0, 2, 1).reshape(blocks, span, groups_local, per_group, 1)
    ).astype(jnp.bfloat16)
    block_states = jnp.einsum(
        "bsghp,bsgn->bghpn", x_weighted, b_blocks, preferred_element_type=jnp.float32
    ).reshape(blocks, heads_local, width, state)
    block_gates = jnp.exp(cum_t[:, :, -1]) * (segment[:, -1] == 0).astype(jnp.float32)[:, None]

    prior_states = [jnp.zeros_like(block_states[0])]
    prior_gates = [jnp.ones_like(block_gates[0])]
    for b in range(1, blocks):
        prior_states.append(block_gates[b - 1][:, None, None] * prior_states[-1] + block_states[b - 1])
        prior_gates.append(prior_gates[-1] * block_gates[b - 1])
    slab_state = block_gates[-1][:, None, None] * prior_states[-1] + block_states[-1]
    slab_gate = prior_gates[-1] * block_gates[-1]
    slab_gate, slab_state, incoming_z = lax.optimization_barrier((slab_gate, slab_state, incoming_z))
    z_pack = placed(incoming_z)
    arriving = chain(slab_gate, slab_state, "ctx")
    entering = (
        (jnp.stack(prior_states) + jnp.stack(prior_gates)[:, :, None, None] * arriving[None])
        .astype(jnp.bfloat16)
        .reshape(blocks, groups_local, per_group, width, state)
    )
    y_off = jnp.einsum("bqgn,bghpn->bqghp", c_blocks, entering, preferred_element_type=jnp.float32)
    reach = (
        (jnp.exp(cum_t) * (segment == 0).astype(jnp.float32)[:, None, :])
        .transpose(0, 2, 1)
        .reshape(blocks, span, groups_local, per_group, 1)
    )
    mixed_y = (
        y_diag
        + y_off * reach
        + skip_gain.reshape(groups_local, per_group, 1) * x_blocks.astype(jnp.float32)
    )
    gated = mixed_y * jax.nn.silu(
        z_pack.astype(jnp.float32).reshape(blocks, span, groups_local, per_group, width)
    )
    power = jnp.mean(gated * gated, axis=(3, 4), keepdims=True)
    normed = (
        (gated * lax.rsqrt(power + eps) * norm_gain.reshape(groups_local, per_group, width))
        .astype(jnp.bfloat16)
        .reshape(rows, heads_local * width)
    )
    partial_value = jnp.dot(normed, out_weight, preferred_element_type=jnp.float32)
    result = lax.psum_scatter(
        partial_value.astype(jnp.bfloat16), "head", scatter_dimension=1, tiled=True
    )
    return result[None]


def solution(mesh):
    return jax.shard_map(
        body,
        mesh=mesh,
        in_specs=(
            P("dp", "ctx", "head"),
            P("dp", "ctx", "head"),
            P("dp", "ctx", "head", None),
            P("dp", "ctx", "head"),
            P("head"),
            P("head"),
            P(None, "head"),
            P(None, "head", None),
            P(),
            P("dp", "ctx"),
            P("head"),
            P("head", None),
        ),
        out_specs=P("dp", "ctx", "head"),
        check_vma=False,
    )
```

```python
import jax
import jax.numpy as jnp
from jax import lax
from jax.sharding import PartitionSpec as P

BLOCK_LEN = 128


eps = 1e-05


def passed_along(block, axis, distance):
    devices = range(lax.axis_size(axis))
    route = [(i - distance, i) for i in devices if i - distance in devices]
    return lax.ppermute(block, axis, route)


def chain(gate, summed, axis):
    count = lax.axis_size(axis)
    place = lax.axis_index(axis)
    core = place % 2
    chip = place // 2
    chips = count // 2
    swap = [(i, i ^ 1) for i in range(count)]

    def join(earlier, latter):
        return (earlier[0] * latter[0], latter[0][:, None, None] * earlier[1] + latter[1])

    def across(pair, route):
        gate_in, summed_in = lax.ppermute((pair[0], pair[1].astype(jnp.bfloat16)), axis, route)
        return gate_in, summed_in.astype(jnp.float32)

    local = (gate, summed)
    other = across(local, swap)
    lead = core == 0
    first = tuple(jnp.where(lead, a, b) for a, b in zip(local, other))
    second = tuple(jnp.where(lead, b, a) for a, b in zip(local, other))
    both = join(first, second)
    half = gate.shape[0] // 2
    mine = tuple(lax.dynamic_slice_in_dim(a, core * half, half, 0) for a in both)

    def fetch(pair, distance):
        gate_in, summed_in = across(pair, [(i - 2 * distance, i) for i in range(2 * distance, count)])
        return jnp.where(chip >= distance, gate_in, 1.0), summed_in

    before = fetch(mine, 1)
    window = join(before, mine)
    distance = 2
    while distance < chips:
        received = fetch(window, distance)
        before = join(received, before)
        distance *= 2
        if distance < chips:
            window = join(received, window)
    partner = across(before, swap)
    whole = tuple(
        jnp.where(lead, jnp.concatenate([a, b]), jnp.concatenate([b, a]))
        for a, b in zip(before, partner)
    )
    return jnp.where(lead, whole[1], join(whole, first)[1])


def conv_core(ext_values, weight, free_ext, length):
    tap_count = weight.shape[0]
    summed = jnp.zeros((length,) + ext_values.shape[1:], jnp.float32)
    keeping = jnp.ones((length,), jnp.float32)
    bshape = (length,) + (1,) * (ext_values.ndim - 1)
    for back in range(tap_count):
        if back > 0:
            keeping = keeping * free_ext[tap_count - back : tap_count - back + length]
        sample = ext_values[tap_count - 1 - back : tap_count - 1 - back + length].astype(
            jnp.float32
        )
        summed = summed + weight[tap_count - 1 - back] * sample * keeping.reshape(bshape)
    return jax.nn.silu(summed).astype(jnp.bfloat16)


def body(
    token_values,
    gate_values,
    state_maps,
    step_raw,
    log_rate,
    skip_gain,
    conv_values,
    conv_maps,
    piece_shift,
    doc_start,
    norm_gain,
    out_weight,
):
    owners = lax.axis_size(("dp", "ctx"))
    myself = lax.axis_index(("dp", "ctx"))
    slots = piece_shift.shape[0]
    rows = token_values.shape[1]
    piece_rows = rows // slots
    most = 2 * slots // owners
    slot_ids = jnp.arange(slots, dtype=jnp.int32)
    matching = piece_shift[:, None] == piece_shift[None, :]
    ranking = jnp.sum(
        (matching & (slot_ids[None, :] < slot_ids[:, None])).astype(jnp.int32), axis=1
    )
    offsets = (jnp.arange(owners, dtype=jnp.int32) - myself) % owners
    chosen = (piece_shift[None, None, :] == offsets[:, None, None]) & (
        ranking[None, None, :] == jnp.arange(most, dtype=jnp.int32)[None, :, None]
    )
    send_slot = jnp.sum(chosen.astype(jnp.int32) * slot_ids[None, None, :], axis=2)

    def outgoing(local):
        pieces = local[0].reshape((slots, piece_rows) + local.shape[2:])
        return pieces[send_slot]

    features = token_values.shape[2]
    map_shape = state_maps.shape[2:]
    map_width = map_shape[0] * map_shape[1]
    joined = jnp.concatenate(
        [token_values[0], state_maps[0].reshape(rows, map_width), step_raw[0]], axis=1
    )
    incoming = lax.all_to_all(
        outgoing(joined[None]), ("dp", "ctx"), split_axis=0, concat_axis=0, tiled=True
    )
    incoming_z = lax.all_to_all(
        outgoing(gate_values), ("dp", "ctx"), split_axis=0, concat_axis=0, tiled=True
    )
    source = (myself - piece_shift) % owners

    def placed(received):
        return received[source, ranking].reshape((rows,) + received.shape[3:])

    joined_pack = placed(incoming)
    margin = conv_values.shape[0] - 1
    flags = doc_start[0].astype(jnp.bfloat16)
    rim = passed_along(
        jnp.concatenate([joined_pack[rows - margin :], flags[rows - margin :, None]], axis=1),
        "ctx",
        1,
    )
    rim_x = rim[:, :features]
    rim_maps = rim[:, features : features + map_width].reshape((margin,) + map_shape)
    rim_flags = rim[:, -1]
    x_pack = joined_pack[:, :features]
    map_pack = joined_pack[:, features : features + map_width].reshape((rows,) + map_shape)
    dt_pack = joined_pack[:, features + map_width :]
    free_ext = 1.0 - jnp.concatenate([rim_flags, flags]).astype(jnp.float32)
    x_conv = conv_core(jnp.concatenate([rim_x, x_pack]), conv_values, free_ext, rows)
    map_conv = conv_core(jnp.concatenate([rim_maps, map_pack]), conv_maps, free_ext, rows)
    heads_local = log_rate.shape[0]
    groups_local = map_pack.shape[1]
    per_group = heads_local // groups_local
    width = x_pack.shape[1] // heads_local
    state = map_pack.shape[2] // 2
    span = BLOCK_LEN
    blocks = rows // span
    step_dt = jax.nn.softplus(dt_pack.astype(jnp.float32))
    log_decay = step_dt * (-jnp.exp(log_rate))[None, :]
    cum_t = jnp.cumsum(log_decay.reshape(blocks, span, heads_local), axis=1).transpose(0, 2, 1)
    dt_t = step_dt.reshape(blocks, span, heads_local).transpose(0, 2, 1)
    segment = jnp.cumsum(doc_start[0].reshape(blocks, span), axis=1)
    x_blocks = x_conv.reshape(blocks, span, groups_local, per_group, width)
    b_blocks = map_conv[:, :, :state].reshape(blocks, span, groups_local, state)
    c_blocks = map_conv[:, :, state:].reshape(blocks, span, groups_local, state)
    scores = jnp.einsum("bqgn,bsgn->bgqs", c_blocks, b_blocks, preferred_element_type=jnp.float32)
    later = jnp.arange(span)[:, None] >= jnp.arange(span)[None, :]
    allowed = later[None] & (segment[:, :, None] == segment[:, None, :])
    spread = cum_t[:, :, :, None] - cum_t[:, :, None, :]
    decay = jnp.exp(jnp.where(allowed[:, None], spread, -jnp.inf))
    weights = (
        decay.reshape(blocks, groups_local, per_group, span, span)
        * scores[:, :, None]
        * dt_t.reshape(blocks, groups_local, per_group, 1, span)
    ).astype(jnp.bfloat16)
    y_diag = jnp.einsum("bghts,bsghp->btghp", weights, x_blocks, preferred_element_type=jnp.float32)
    same_end = (segment == segment[:, -1:]).astype(jnp.float32)
    carry_coef = jnp.exp(cum_t[:, :, -1:] - cum_t) * dt_t * same_end[:, None, :]
    x_weighted = (
        x_blocks.astype(jnp.float32)
        * carry_coef.transpose(0, 2, 1).reshape(blocks, span, groups_local, per_group, 1)
    ).astype(jnp.bfloat16)
    block_states = jnp.einsum(
        "bsghp,bsgn->bghpn", x_weighted, b_blocks, preferred_element_type=jnp.float32
    ).reshape(blocks, heads_local, width, state)
    block_gates = jnp.exp(cum_t[:, :, -1]) * (segment[:, -1] == 0).astype(jnp.float32)[:, None]

    prior_states = [jnp.zeros_like(block_states[0])]
    prior_gates = [jnp.ones_like(block_gates[0])]
    for b in range(1, blocks):
        prior_states.append(block_gates[b - 1][:, None, None] * prior_states[-1] + block_states[b - 1])
        prior_gates.append(prior_gates[-1] * block_gates[b - 1])
    slab_state = block_gates[-1][:, None, None] * prior_states[-1] + block_states[-1]
    slab_gate = prior_gates[-1] * block_gates[-1]
    slab_gate, slab_state, incoming_z = lax.optimization_barrier((slab_gate, slab_state, incoming_z))
    z_pack = placed(incoming_z)
    arriving = chain(slab_gate, slab_state, "ctx")
    entering = (
        (jnp.stack(prior_states) + jnp.stack(prior_gates)[:, :, None, None] * arriving[None])
        .astype(jnp.bfloat16)
        .reshape(blocks, groups_local, per_group, width, state)
    )
    y_off = jnp.einsum("bqgn,bghpn->bqghp", c_blocks, entering, preferred_element_type=jnp.float32)
    reach = (
        (jnp.exp(cum_t) * (segment == 0).astype(jnp.float32)[:, None, :])
        .transpose(0, 2, 1)
        .reshape(blocks, span, groups_local, per_group, 1)
    )
    mixed_y = (
        y_diag
        + y_off * reach
        + skip_gain.reshape(groups_local, per_group, 1) * x_blocks.astype(jnp.float32)
    )
    gated = mixed_y * jax.nn.silu(
        z_pack.astype(jnp.float32).reshape(blocks, span, groups_local, per_group, width)
    )
    power = jnp.mean(gated * gated, axis=(3, 4), keepdims=True)
    normed = (
        (gated * lax.rsqrt(power + eps) * norm_gain.reshape(groups_local, per_group, width))
        .astype(jnp.bfloat16)
        .reshape(rows, heads_local * width)
    )
    partial_value = jnp.dot(normed, out_weight, preferred_element_type=jnp.float32)
    result = lax.psum_scatter(
        partial_value.astype(jnp.bfloat16), "head", scatter_dimension=1, tiled=True
    )
    return result[None]


def solution(mesh):
    return jax.shard_map(
        body,
        mesh=mesh,
        in_specs=(
            P("dp", "ctx", "head"),
            P("dp", "ctx", "head"),
            P("dp", "ctx", "head", None),
            P("dp", "ctx", "head"),
            P("head"),
            P("head"),
            P(None, "head"),
            P(None, "head", None),
            P(),
            P("dp", "ctx"),
            P("head"),
            P("head", None),
        ),
        out_specs=P("dp", "ctx", "head"),
        check_vma=False,
    )
```

```python
import jax
import jax.numpy as jnp
from jax import lax
from jax.sharding import PartitionSpec as P

BLOCK_LEN = 128


eps = 1e-05


def passed_along(block, axis, distance):
    devices = range(lax.axis_size(axis))
    route = [(i - distance, i) for i in devices if i - distance in devices]
    return lax.ppermute(block, axis, route)


def chain(gate, summed, axis):
    count = lax.axis_size(axis)
    place = lax.axis_index(axis)
    core = place % 2
    chip = place // 2
    chips = count // 2
    swap = [(i, i ^ 1) for i in range(count)]

    def join(earlier, latter):
        return (earlier[0] * latter[0], latter[0][:, None, None] * earlier[1] + latter[1])

    def across(pair, route):
        gate_in, summed_in = lax.ppermute((pair[0], pair[1].astype(jnp.bfloat16)), axis, route)
        return gate_in, summed_in.astype(jnp.float32)

    local = (gate, summed)
    other = across(local, swap)
    lead = core == 0
    first = tuple(jnp.where(lead, a, b) for a, b in zip(local, other))
    second = tuple(jnp.where(lead, b, a) for a, b in zip(local, other))
    both = join(first, second)
    half = gate.shape[0] // 2
    mine = tuple(lax.dynamic_slice_in_dim(a, core * half, half, 0) for a in both)

    def fetch(pair, distance):
        gate_in, summed_in = across(pair, [(i - 2 * distance, i) for i in range(2 * distance, count)])
        return jnp.where(chip >= distance, gate_in, 1.0), summed_in

    before = fetch(mine, 1)
    window = join(before, mine)
    distance = 2
    while distance < chips:
        received = fetch(window, distance)
        before = join(received, before)
        distance *= 2
        if distance < chips:
            window = join(received, window)
    partner = across(before, swap)
    whole = tuple(
        jnp.where(lead, jnp.concatenate([a, b]), jnp.concatenate([b, a]))
        for a, b in zip(before, partner)
    )
    return jnp.where(lead, whole[1], join(whole, first)[1])


def conv_core(ext_values, weight, free_ext, length):
    tap_count = weight.shape[0]
    summed = jnp.zeros((length,) + ext_values.shape[1:], jnp.float32)
    keeping = jnp.ones((length,), jnp.float32)
    bshape = (length,) + (1,) * (ext_values.ndim - 1)
    for back in range(tap_count):
        if back > 0:
            keeping = keeping * free_ext[tap_count - back : tap_count - back + length]
        sample = ext_values[tap_count - 1 - back : tap_count - 1 - back + length].astype(
            jnp.float32
        )
        summed = summed + weight[tap_count - 1 - back] * sample * keeping.reshape(bshape)
    return jax.nn.silu(summed).astype(jnp.bfloat16)


def body(
    token_values,
    gate_values,
    state_maps,
    step_raw,
    log_rate,
    skip_gain,
    conv_values,
    conv_maps,
    piece_shift,
    doc_start,
    norm_gain,
    out_weight,
):
    owners = lax.axis_size(("dp", "ctx"))
    myself = lax.axis_index(("dp", "ctx"))
    slots = piece_shift.shape[0]
    rows = token_values.shape[1]
    piece_rows = rows // slots
    most = 2 * slots // owners
    slot_ids = jnp.arange(slots, dtype=jnp.int32)
    matching = piece_shift[:, None] == piece_shift[None, :]
    ranking = jnp.sum(
        (matching & (slot_ids[None, :] < slot_ids[:, None])).astype(jnp.int32), axis=1
    )
    offsets = (jnp.arange(owners, dtype=jnp.int32) - myself) % owners
    chosen = (piece_shift[None, None, :] == offsets[:, None, None]) & (
        ranking[None, None, :] == jnp.arange(most, dtype=jnp.int32)[None, :, None]
    )
    send_slot = jnp.sum(chosen.astype(jnp.int32) * slot_ids[None, None, :], axis=2)

    def outgoing(local):
        pieces = local[0].reshape((slots, piece_rows) + local.shape[2:])
        return pieces[send_slot]

    features = token_values.shape[2]
    map_shape = state_maps.shape[2:]
    map_width = map_shape[0] * map_shape[1]
    joined = jnp.concatenate(
        [token_values[0], state_maps[0].reshape(rows, map_width), step_raw[0]], axis=1
    )
    incoming = lax.all_to_all(
        outgoing(joined[None]), ("dp", "ctx"), split_axis=0, concat_axis=0, tiled=True
    )
    incoming_z = lax.all_to_all(
        outgoing(gate_values), ("dp", "ctx"), split_axis=0, concat_axis=0, tiled=True
    )
    source = (myself - piece_shift) % owners

    def placed(received):
        return received[source, ranking].reshape((rows,) + received.shape[3:])

    joined_pack = placed(incoming)
    margin = conv_values.shape[0] - 1
    flags = doc_start[0].astype(jnp.bfloat16)
    rim = passed_along(
        jnp.concatenate([joined_pack[rows - margin :], flags[rows - margin :, None]], axis=1),
        "ctx",
        1,
    )
    rim_x = rim[:, :features]
    rim_maps = rim[:, features : features + map_width].reshape((margin,) + map_shape)
    rim_flags = rim[:, -1]
    x_pack = joined_pack[:, :features]
    map_pack = joined_pack[:, features : features + map_width].reshape((rows,) + map_shape)
    dt_pack = joined_pack[:, features + map_width :]
    free_ext = 1.0 - jnp.concatenate([rim_flags, flags]).astype(jnp.float32)
    x_conv = conv_core(jnp.concatenate([rim_x, x_pack]), conv_values, free_ext, rows)
    map_conv = conv_core(jnp.concatenate([rim_maps, map_pack]), conv_maps, free_ext, rows)
    heads_local = log_rate.shape[0]
    groups_local = map_pack.shape[1]
    per_group = heads_local // groups_local
    width = x_pack.shape[1] // heads_local
    state = map_pack.shape[2] // 2
    span = BLOCK_LEN
    blocks = rows // span
    step_dt = jax.nn.softplus(dt_pack.astype(jnp.float32))
    log_decay = step_dt * (-jnp.exp(log_rate))[None, :]
    cum_t = jnp.cumsum(log_decay.reshape(blocks, span, heads_local), axis=1).transpose(0, 2, 1)
    dt_t = step_dt.reshape(blocks, span, heads_local).transpose(0, 2, 1)
    segment = jnp.cumsum(doc_start[0].reshape(blocks, span), axis=1)
    x_blocks = x_conv.reshape(blocks, span, groups_local, per_group, width)
    b_blocks = map_conv[:, :, :state].reshape(blocks, span, groups_local, state)
    c_blocks = map_conv[:, :, state:].reshape(blocks, span, groups_local, state)
    scores = jnp.einsum("bqgn,bsgn->bgqs", c_blocks, b_blocks, preferred_element_type=jnp.float32)
    later = jnp.arange(span)[:, None] >= jnp.arange(span)[None, :]
    allowed = later[None] & (segment[:, :, None] == segment[:, None, :])
    spread = cum_t[:, :, :, None] - cum_t[:, :, None, :]
    decay = jnp.exp(jnp.where(allowed[:, None], spread, -jnp.inf))
    weights = (
        decay.reshape(blocks, groups_local, per_group, span, span)
        * scores[:, :, None]
        * dt_t.reshape(blocks, groups_local, per_group, 1, span)
    ).astype(jnp.bfloat16)
    y_diag = jnp.einsum("bghts,bsghp->btghp", weights, x_blocks, preferred_element_type=jnp.float32)
    same_end = (segment == segment[:, -1:]).astype(jnp.float32)
    carry_coef = jnp.exp(cum_t[:, :, -1:] - cum_t) * dt_t * same_end[:, None, :]
    x_weighted = (
        x_blocks.astype(jnp.float32)
        * carry_coef.transpose(0, 2, 1).reshape(blocks, span, groups_local, per_group, 1)
    ).astype(jnp.bfloat16)
    block_states = jnp.einsum(
        "bsghp,bsgn->bghpn", x_weighted, b_blocks, preferred_element_type=jnp.float32
    ).reshape(blocks, heads_local, width, state)
    block_gates = jnp.exp(cum_t[:, :, -1]) * (segment[:, -1] == 0).astype(jnp.float32)[:, None]

    prior_states = [jnp.zeros_like(block_states[0])]
    prior_gates = [jnp.ones_like(block_gates[0])]
    for b in range(1, blocks):
        prior_states.append(block_gates[b - 1][:, None, None] * prior_states[-1] + block_states[b - 1])
        prior_gates.append(prior_gates[-1] * block_gates[b - 1])
    slab_state = block_gates[-1][:, None, None] * prior_states[-1] + block_states[-1]
    slab_gate = prior_gates[-1] * block_gates[-1]
    z_pack = placed(incoming_z)
    arriving = chain(slab_gate, slab_state, "ctx")
    entering = (
        (jnp.stack(prior_states) + jnp.stack(prior_gates)[:, :, None, None] * arriving[None])
        .astype(jnp.bfloat16)
        .reshape(blocks, groups_local, per_group, width, state)
    )
    y_off = jnp.einsum("bqgn,bghpn->bqghp", c_blocks, entering, preferred_element_type=jnp.float32)
    reach = (
        (jnp.exp(cum_t) * (segment == 0).astype(jnp.float32)[:, None, :])
        .transpose(0, 2, 1)
        .reshape(blocks, span, groups_local, per_group, 1)
    )
    mixed_y = (
        y_diag
        + y_off * reach
        + skip_gain.reshape(groups_local, per_group, 1) * x_blocks.astype(jnp.float32)
    )
    gated = mixed_y * jax.nn.silu(
        z_pack.astype(jnp.float32).reshape(blocks, span, groups_local, per_group, width)
    )
    power = jnp.mean(gated * gated, axis=(3, 4), keepdims=True)
    normed = (
        (gated * lax.rsqrt(power + eps) * norm_gain.reshape(groups_local, per_group, width))
        .astype(jnp.bfloat16)
        .reshape(rows, heads_local * width)
    )
    partial_value = jnp.dot(normed, out_weight, preferred_element_type=jnp.float32)
    result = lax.psum_scatter(
        partial_value.astype(jnp.bfloat16), "head", scatter_dimension=1, tiled=True
    )
    return result[None]


def solution(mesh):
    return jax.shard_map(
        body,
        mesh=mesh,
        in_specs=(
            P("dp", "ctx", "head"),
            P("dp", "ctx", "head"),
            P("dp", "ctx", "head", None),
            P("dp", "ctx", "head"),
            P("head"),
            P("head"),
            P(None, "head"),
            P(None, "head", None),
            P(),
            P("dp", "ctx"),
            P("head"),
            P("head", None),
        ),
        out_specs=P("dp", "ctx", "head"),
        check_vma=False,
    )
```

```python
import jax
import jax.numpy as jnp
from jax import lax
from jax.sharding import PartitionSpec as P

BLOCK_LEN = 128


eps = 1e-05


def passed_along(block, axis, distance):
    devices = range(lax.axis_size(axis))
    route = [(i - distance, i) for i in devices if i - distance in devices]
    return lax.ppermute(block, axis, route)


def chain(gate, summed, axis):
    count = lax.axis_size(axis)
    place = lax.axis_index(axis)
    core = place % 2
    chip = place // 2
    chips = count // 2
    swap = [(i, i ^ 1) for i in range(count)]

    def join(earlier, latter):
        return (earlier[0] * latter[0], latter[0][:, None, None] * earlier[1] + latter[1])

    def across(pair, route):
        gate_in, summed_in = lax.ppermute((pair[0], pair[1].astype(jnp.bfloat16)), axis, route)
        return gate_in, summed_in.astype(jnp.float32)

    local = (gate, summed)
    other = across(local, swap)
    lead = core == 0
    first = tuple(jnp.where(lead, a, b) for a, b in zip(local, other))
    second = tuple(jnp.where(lead, b, a) for a, b in zip(local, other))
    both = join(first, second)
    half = gate.shape[0] // 2
    mine = tuple(lax.dynamic_slice_in_dim(a, core * half, half, 0) for a in both)

    def fetch(pair, distance):
        gate_in, summed_in = across(pair, [(i - 2 * distance, i) for i in range(2 * distance, count)])
        return jnp.where(chip >= distance, gate_in, 1.0), summed_in

    before = fetch(mine, 1)
    window = join(before, mine)
    distance = 2
    while distance < chips:
        received = fetch(window, distance)
        before = join(received, before)
        distance *= 2
        if distance < chips:
            window = join(received, window)
    partner = across(before, swap)
    whole = tuple(
        jnp.where(lead, jnp.concatenate([a, b]), jnp.concatenate([b, a]))
        for a, b in zip(before, partner)
    )
    return jnp.where(lead, whole[1], join(whole, first)[1])


def conv_core(ext_values, weight, free_ext, length):
    tap_count = weight.shape[0]
    summed = jnp.zeros((length,) + ext_values.shape[1:], jnp.float32)
    keeping = jnp.ones((length,), jnp.float32)
    bshape = (length,) + (1,) * (ext_values.ndim - 1)
    for back in range(tap_count):
        if back > 0:
            keeping = keeping * free_ext[tap_count - back : tap_count - back + length]
        sample = ext_values[tap_count - 1 - back : tap_count - 1 - back + length].astype(
            jnp.float32
        )
        summed = summed + weight[tap_count - 1 - back] * sample * keeping.reshape(bshape)
    return jax.nn.silu(summed).astype(jnp.bfloat16)


def body(
    token_values,
    gate_values,
    state_maps,
    step_raw,
    log_rate,
    skip_gain,
    conv_values,
    conv_maps,
    piece_shift,
    doc_start,
    norm_gain,
    out_weight,
):
    owners = lax.axis_size(("dp", "ctx"))
    myself = lax.axis_index(("dp", "ctx"))
    slots = piece_shift.shape[0]
    rows = token_values.shape[1]
    piece_rows = rows // slots
    most = 2 * slots // owners
    slot_ids = jnp.arange(slots, dtype=jnp.int32)
    matching = piece_shift[:, None] == piece_shift[None, :]
    ranking = jnp.sum(
        (matching & (slot_ids[None, :] < slot_ids[:, None])).astype(jnp.int32), axis=1
    )
    offsets = (jnp.arange(owners, dtype=jnp.int32) - myself) % owners
    chosen = (piece_shift[None, None, :] == offsets[:, None, None]) & (
        ranking[None, None, :] == jnp.arange(most, dtype=jnp.int32)[None, :, None]
    )
    send_slot = jnp.sum(chosen.astype(jnp.int32) * slot_ids[None, None, :], axis=2)

    def outgoing(local):
        pieces = local[0].reshape((slots, piece_rows) + local.shape[2:])
        return pieces[send_slot]

    features = token_values.shape[2]
    map_shape = state_maps.shape[2:]
    map_width = map_shape[0] * map_shape[1]
    joined = jnp.concatenate(
        [token_values[0], state_maps[0].reshape(rows, map_width), step_raw[0]], axis=1
    )
    incoming = lax.all_to_all(
        outgoing(joined[None]), ("dp", "ctx"), split_axis=0, concat_axis=0, tiled=True
    )
    incoming_z = lax.all_to_all(
        outgoing(gate_values), ("dp", "ctx"), split_axis=0, concat_axis=0, tiled=True
    )
    source = (myself - piece_shift) % owners

    def placed(received):
        return received[source, ranking].reshape((rows,) + received.shape[3:])

    joined_pack = placed(incoming)
    margin = conv_values.shape[0] - 1
    flags = doc_start[0].astype(jnp.bfloat16)
    edges = lax.all_gather(
        jnp.concatenate([joined[rows - margin :], flags[rows - margin :, None]], axis=1),
        ("dp", "ctx"),
    )
    earlier = lax.axis_index("ctx") > 0
    rim = jnp.concatenate(
        [
            edges[(myself - 1 - piece_shift[slots - 1]) % owners, :, :-1],
            edges[(myself - 1) % owners, :, -1:],
        ],
        axis=1,
    )
    rim = jnp.where(earlier, rim, jnp.zeros_like(rim))
    rim_x = rim[:, :features]
    rim_maps = rim[:, features : features + map_width].reshape((margin,) + map_shape)
    rim_flags = rim[:, -1]
    x_pack = joined_pack[:, :features]
    map_pack = joined_pack[:, features : features + map_width].reshape((rows,) + map_shape)
    dt_pack = joined_pack[:, features + map_width :]
    free_ext = 1.0 - jnp.concatenate([rim_flags, flags]).astype(jnp.float32)
    x_conv = conv_core(jnp.concatenate([rim_x, x_pack]), conv_values, free_ext, rows)
    map_conv = conv_core(jnp.concatenate([rim_maps, map_pack]), conv_maps, free_ext, rows)
    heads_local = log_rate.shape[0]
    groups_local = map_pack.shape[1]
    per_group = heads_local // groups_local
    width = x_pack.shape[1] // heads_local
    state = map_pack.shape[2] // 2
    span = BLOCK_LEN
    blocks = rows // span
    step_dt = jax.nn.softplus(dt_pack.astype(jnp.float32))
    log_decay = step_dt * (-jnp.exp(log_rate))[None, :]
    cum_t = jnp.cumsum(log_decay.reshape(blocks, span, heads_local), axis=1).transpose(0, 2, 1)
    dt_t = step_dt.reshape(blocks, span, heads_local).transpose(0, 2, 1)
    segment = jnp.cumsum(doc_start[0].reshape(blocks, span), axis=1)
    x_blocks = x_conv.reshape(blocks, span, groups_local, per_group, width)
    b_blocks = map_conv[:, :, :state].reshape(blocks, span, groups_local, state)
    c_blocks = map_conv[:, :, state:].reshape(blocks, span, groups_local, state)
    scores = jnp.einsum("bqgn,bsgn->bgqs", c_blocks, b_blocks, preferred_element_type=jnp.float32)
    later = jnp.arange(span)[:, None] >= jnp.arange(span)[None, :]
    allowed = later[None] & (segment[:, :, None] == segment[:, None, :])
    spread = cum_t[:, :, :, None] - cum_t[:, :, None, :]
    decay = jnp.exp(jnp.where(allowed[:, None], spread, -jnp.inf))
    weights = (
        decay.reshape(blocks, groups_local, per_group, span, span)
        * scores[:, :, None]
        * dt_t.reshape(blocks, groups_local, per_group, 1, span)
    ).astype(jnp.bfloat16)
    y_diag = jnp.einsum("bghts,bsghp->btghp", weights, x_blocks, preferred_element_type=jnp.float32)
    same_end = (segment == segment[:, -1:]).astype(jnp.float32)
    carry_coef = jnp.exp(cum_t[:, :, -1:] - cum_t) * dt_t * same_end[:, None, :]
    x_weighted = (
        x_blocks.astype(jnp.float32)
        * carry_coef.transpose(0, 2, 1).reshape(blocks, span, groups_local, per_group, 1)
    ).astype(jnp.bfloat16)
    block_states = jnp.einsum(
        "bsghp,bsgn->bghpn", x_weighted, b_blocks, preferred_element_type=jnp.float32
    ).reshape(blocks, heads_local, width, state)
    block_gates = jnp.exp(cum_t[:, :, -1]) * (segment[:, -1] == 0).astype(jnp.float32)[:, None]

    prior_states = [jnp.zeros_like(block_states[0])]
    prior_gates = [jnp.ones_like(block_gates[0])]
    for b in range(1, blocks):
        prior_states.append(block_gates[b - 1][:, None, None] * prior_states[-1] + block_states[b - 1])
        prior_gates.append(prior_gates[-1] * block_gates[b - 1])
    slab_state = block_gates[-1][:, None, None] * prior_states[-1] + block_states[-1]
    slab_gate = prior_gates[-1] * block_gates[-1]
    z_pack = placed(incoming_z)
    arriving = chain(slab_gate, slab_state, "ctx")
    entering = (
        (jnp.stack(prior_states) + jnp.stack(prior_gates)[:, :, None, None] * arriving[None])
        .astype(jnp.bfloat16)
        .reshape(blocks, groups_local, per_group, width, state)
    )
    y_off = jnp.einsum("bqgn,bghpn->bqghp", c_blocks, entering, preferred_element_type=jnp.float32)
    reach = (
        (jnp.exp(cum_t) * (segment == 0).astype(jnp.float32)[:, None, :])
        .transpose(0, 2, 1)
        .reshape(blocks, span, groups_local, per_group, 1)
    )
    mixed_y = (
        y_diag
        + y_off * reach
        + skip_gain.reshape(groups_local, per_group, 1) * x_blocks.astype(jnp.float32)
    )
    gated = mixed_y * jax.nn.silu(
        z_pack.astype(jnp.float32).reshape(blocks, span, groups_local, per_group, width)
    )
    power = jnp.mean(gated * gated, axis=(3, 4), keepdims=True)
    normed = (
        (gated * lax.rsqrt(power + eps) * norm_gain.reshape(groups_local, per_group, width))
        .astype(jnp.bfloat16)
        .reshape(rows, heads_local * width)
    )
    partial_value = jnp.dot(normed, out_weight, preferred_element_type=jnp.float32)
    result = lax.psum_scatter(
        partial_value.astype(jnp.bfloat16), "head", scatter_dimension=1, tiled=True
    )
    return result[None]


def solution(mesh):
    return jax.shard_map(
        body,
        mesh=mesh,
        in_specs=(
            P("dp", "ctx", "head"),
            P("dp", "ctx", "head"),
            P("dp", "ctx", "head", None),
            P("dp", "ctx", "head"),
            P("head"),
            P("head"),
            P(None, "head"),
            P(None, "head", None),
            P(),
            P("dp", "ctx"),
            P("head"),
            P("head", None),
        ),
        out_specs=P("dp", "ctx", "head"),
        check_vma=False,
    )
```

```python
import jax
import jax.numpy as jnp
from jax import lax
from jax.sharding import PartitionSpec as P

BLOCK_LEN = 128


eps = 1e-05


def passed_along(block, axis, distance):
    devices = range(lax.axis_size(axis))
    route = [(i - distance, i) for i in devices if i - distance in devices]
    return lax.ppermute(block, axis, route)


def chain(gate, summed, axis):
    count = lax.axis_size(axis)
    place = lax.axis_index(axis)
    core = place % 2
    chip = place // 2
    chips = count // 2
    swap = [(i, i ^ 1) for i in range(count)]

    def join(earlier, latter):
        return (earlier[0] * latter[0], latter[0][:, None, None] * earlier[1] + latter[1])

    def across(pair, route):
        gate_in, summed_in = lax.ppermute((pair[0], pair[1].astype(jnp.bfloat16)), axis, route)
        return gate_in, summed_in.astype(jnp.float32)

    local = (gate, summed)
    other = across(local, swap)
    lead = core == 0
    first = tuple(jnp.where(lead, a, b) for a, b in zip(local, other))
    second = tuple(jnp.where(lead, b, a) for a, b in zip(local, other))
    both = join(first, second)
    half = gate.shape[0] // 2
    mine = tuple(lax.dynamic_slice_in_dim(a, core * half, half, 0) for a in both)

    def fetch(pair, distance):
        gate_in, summed_in = across(pair, [(i - 2 * distance, i) for i in range(2 * distance, count)])
        return jnp.where(chip >= distance, gate_in, 1.0), summed_in

    before = fetch(mine, 1)
    window = join(before, mine)
    distance = 2
    while distance < chips:
        received = fetch(window, distance)
        before = join(received, before)
        distance *= 2
        if distance < chips:
            window = join(received, window)
    partner = across(before, swap)
    whole = tuple(
        jnp.where(lead, jnp.concatenate([a, b]), jnp.concatenate([b, a]))
        for a, b in zip(before, partner)
    )
    return jnp.where(lead, whole[1], join(whole, first)[1])


def conv_core(ext_values, weight, free_ext, length):
    tap_count = weight.shape[0]
    summed = jnp.zeros((length,) + ext_values.shape[1:], jnp.float32)
    keeping = jnp.ones((length,), jnp.float32)
    bshape = (length,) + (1,) * (ext_values.ndim - 1)
    for back in range(tap_count):
        if back > 0:
            keeping = keeping * free_ext[tap_count - back : tap_count - back + length]
        sample = ext_values[tap_count - 1 - back : tap_count - 1 - back + length].astype(
            jnp.float32
        )
        summed = summed + weight[tap_count - 1 - back] * sample * keeping.reshape(bshape)
    return jax.nn.silu(summed).astype(jnp.bfloat16)


def body(
    token_values,
    gate_values,
    state_maps,
    step_raw,
    log_rate,
    skip_gain,
    conv_values,
    conv_maps,
    piece_shift,
    doc_start,
    norm_gain,
    out_weight,
):
    owners = lax.axis_size(("dp", "ctx"))
    myself = lax.axis_index(("dp", "ctx"))
    slots = piece_shift.shape[0]
    rows = token_values.shape[1]
    piece_rows = rows // slots
    most = 2 * slots // owners
    slot_ids = jnp.arange(slots, dtype=jnp.int32)
    matching = piece_shift[:, None] == piece_shift[None, :]
    ranking = jnp.sum(
        (matching & (slot_ids[None, :] < slot_ids[:, None])).astype(jnp.int32), axis=1
    )
    offsets = (jnp.arange(owners, dtype=jnp.int32) - myself) % owners
    chosen = (piece_shift[None, None, :] == offsets[:, None, None]) & (
        ranking[None, None, :] == jnp.arange(most, dtype=jnp.int32)[None, :, None]
    )
    send_slot = jnp.sum(chosen.astype(jnp.int32) * slot_ids[None, None, :], axis=2)

    def outgoing(local):
        pieces = local[0].reshape((slots, piece_rows) + local.shape[2:])
        return pieces[send_slot]

    features = token_values.shape[2]
    map_shape = state_maps.shape[2:]
    map_width = map_shape[0] * map_shape[1]
    joined = jnp.concatenate(
        [token_values[0], state_maps[0].reshape(rows, map_width), step_raw[0]], axis=1
    )
    margin = conv_values.shape[0] - 1
    flags = doc_start[0].astype(jnp.bfloat16)
    edges = lax.all_gather(
        jnp.concatenate(
            [
                token_values[0, rows - margin :],
                state_maps[0, rows - margin :].reshape(margin, map_width),
                step_raw[0, rows - margin :],
                flags[rows - margin :, None],
            ],
            axis=1,
        ),
        ("dp", "ctx"),
    )
    edges, joined = lax.optimization_barrier((edges, joined))
    incoming = lax.all_to_all(
        outgoing(joined[None]), ("dp", "ctx"), split_axis=0, concat_axis=0, tiled=True
    )
    incoming_z = lax.all_to_all(
        outgoing(gate_values), ("dp", "ctx"), split_axis=0, concat_axis=0, tiled=True
    )
    source = (myself - piece_shift) % owners

    def placed(received):
        return received[source, ranking].reshape((rows,) + received.shape[3:])

    joined_pack = placed(incoming)
    earlier = lax.axis_index("ctx") > 0
    rim = jnp.concatenate(
        [
            edges[(myself - 1 - piece_shift[slots - 1]) % owners, :, :-1],
            edges[(myself - 1) % owners, :, -1:],
        ],
        axis=1,
    )
    rim = jnp.where(earlier, rim, jnp.zeros_like(rim))
    rim_x = rim[:, :features]
    rim_maps = rim[:, features : features + map_width].reshape((margin,) + map_shape)
    rim_flags = rim[:, -1]
    x_pack = joined_pack[:, :features]
    map_pack = joined_pack[:, features : features + map_width].reshape((rows,) + map_shape)
    dt_pack = joined_pack[:, features + map_width :]
    free_ext = 1.0 - jnp.concatenate([rim_flags, flags]).astype(jnp.float32)
    x_conv = conv_core(jnp.concatenate([rim_x, x_pack]), conv_values, free_ext, rows)
    map_conv = conv_core(jnp.concatenate([rim_maps, map_pack]), conv_maps, free_ext, rows)
    heads_local = log_rate.shape[0]
    groups_local = map_pack.shape[1]
    per_group = heads_local // groups_local
    width = x_pack.shape[1] // heads_local
    state = map_pack.shape[2] // 2
    span = BLOCK_LEN
    blocks = rows // span
    step_dt = jax.nn.softplus(dt_pack.astype(jnp.float32))
    log_decay = step_dt * (-jnp.exp(log_rate))[None, :]
    cum_t = jnp.cumsum(log_decay.reshape(blocks, span, heads_local), axis=1).transpose(0, 2, 1)
    dt_t = step_dt.reshape(blocks, span, heads_local).transpose(0, 2, 1)
    segment = jnp.cumsum(doc_start[0].reshape(blocks, span), axis=1)
    x_blocks = x_conv.reshape(blocks, span, groups_local, per_group, width)
    b_blocks = map_conv[:, :, :state].reshape(blocks, span, groups_local, state)
    c_blocks = map_conv[:, :, state:].reshape(blocks, span, groups_local, state)
    scores = jnp.einsum("bqgn,bsgn->bgqs", c_blocks, b_blocks, preferred_element_type=jnp.float32)
    later = jnp.arange(span)[:, None] >= jnp.arange(span)[None, :]
    allowed = later[None] & (segment[:, :, None] == segment[:, None, :])
    spread = cum_t[:, :, :, None] - cum_t[:, :, None, :]
    decay = jnp.exp(jnp.where(allowed[:, None], spread, -jnp.inf))
    weights = (
        decay.reshape(blocks, groups_local, per_group, span, span)
        * scores[:, :, None]
        * dt_t.reshape(blocks, groups_local, per_group, 1, span)
    ).astype(jnp.bfloat16)
    y_diag = jnp.einsum("bghts,bsghp->btghp", weights, x_blocks, preferred_element_type=jnp.float32)
    same_end = (segment == segment[:, -1:]).astype(jnp.float32)
    carry_coef = jnp.exp(cum_t[:, :, -1:] - cum_t) * dt_t * same_end[:, None, :]
    x_weighted = (
        x_blocks.astype(jnp.float32)
        * carry_coef.transpose(0, 2, 1).reshape(blocks, span, groups_local, per_group, 1)
    ).astype(jnp.bfloat16)
    block_states = jnp.einsum(
        "bsghp,bsgn->bghpn", x_weighted, b_blocks, preferred_element_type=jnp.float32
    ).reshape(blocks, heads_local, width, state)
    block_gates = jnp.exp(cum_t[:, :, -1]) * (segment[:, -1] == 0).astype(jnp.float32)[:, None]

    prior_states = [jnp.zeros_like(block_states[0])]
    prior_gates = [jnp.ones_like(block_gates[0])]
    for b in range(1, blocks):
        prior_states.append(block_gates[b - 1][:, None, None] * prior_states[-1] + block_states[b - 1])
        prior_gates.append(prior_gates[-1] * block_gates[b - 1])
    slab_state = block_gates[-1][:, None, None] * prior_states[-1] + block_states[-1]
    slab_gate = prior_gates[-1] * block_gates[-1]
    z_pack = placed(incoming_z)
    arriving = chain(slab_gate, slab_state, "ctx")
    entering = (
        (jnp.stack(prior_states) + jnp.stack(prior_gates)[:, :, None, None] * arriving[None])
        .astype(jnp.bfloat16)
        .reshape(blocks, groups_local, per_group, width, state)
    )
    y_off = jnp.einsum("bqgn,bghpn->bqghp", c_blocks, entering, preferred_element_type=jnp.float32)
    reach = (
        (jnp.exp(cum_t) * (segment == 0).astype(jnp.float32)[:, None, :])
        .transpose(0, 2, 1)
        .reshape(blocks, span, groups_local, per_group, 1)
    )
    mixed_y = (
        y_diag
        + y_off * reach
        + skip_gain.reshape(groups_local, per_group, 1) * x_blocks.astype(jnp.float32)
    )
    gated = mixed_y * jax.nn.silu(
        z_pack.astype(jnp.float32).reshape(blocks, span, groups_local, per_group, width)
    )
    power = jnp.mean(gated * gated, axis=(3, 4), keepdims=True)
    normed = (
        (gated * lax.rsqrt(power + eps) * norm_gain.reshape(groups_local, per_group, width))
        .astype(jnp.bfloat16)
        .reshape(rows, heads_local * width)
    )
    partial_value = jnp.dot(normed, out_weight, preferred_element_type=jnp.float32)
    result = lax.psum_scatter(
        partial_value.astype(jnp.bfloat16), "head", scatter_dimension=1, tiled=True
    )
    return result[None]


def solution(mesh):
    return jax.shard_map(
        body,
        mesh=mesh,
        in_specs=(
            P("dp", "ctx", "head"),
            P("dp", "ctx", "head"),
            P("dp", "ctx", "head", None),
            P("dp", "ctx", "head"),
            P("head"),
            P("head"),
            P(None, "head"),
            P(None, "head", None),
            P(),
            P("dp", "ctx"),
            P("head"),
            P("head", None),
        ),
        out_specs=P("dp", "ctx", "head"),
        check_vma=False,
    )
```

```python
import jax
import jax.numpy as jnp
from jax import lax
from jax.sharding import PartitionSpec as P

BLOCK_LEN = 128


eps = 1e-05


def passed_along(block, axis, distance):
    devices = range(lax.axis_size(axis))
    route = [(i - distance, i) for i in devices if i - distance in devices]
    return lax.ppermute(block, axis, route)


def chain(gate, summed, axis):
    count = lax.axis_size(axis)
    place = lax.axis_index(axis)
    core = place % 2
    chip = place // 2
    chips = count // 2
    swap = [(i, i ^ 1) for i in range(count)]

    def join(earlier, latter):
        return (earlier[0] * latter[0], latter[0][:, None, None] * earlier[1] + latter[1])

    def across(pair, route):
        gate_in, summed_in = lax.ppermute((pair[0], pair[1].astype(jnp.bfloat16)), axis, route)
        return gate_in, summed_in.astype(jnp.float32)

    local = (gate, summed)
    other = across(local, swap)
    lead = core == 0
    first = tuple(jnp.where(lead, a, b) for a, b in zip(local, other))
    second = tuple(jnp.where(lead, b, a) for a, b in zip(local, other))
    both = join(first, second)
    half = gate.shape[0] // 2
    mine = tuple(lax.dynamic_slice_in_dim(a, core * half, half, 0) for a in both)

    def fetch(pair, distance):
        gate_in, summed_in = across(pair, [(i - 2 * distance, i) for i in range(2 * distance, count)])
        return jnp.where(chip >= distance, gate_in, 1.0), summed_in

    before = fetch(mine, 1)
    window = join(before, mine)
    distance = 2
    while distance < chips:
        received = fetch(window, distance)
        before = join(received, before)
        distance *= 2
        if distance < chips:
            window = join(received, window)
    partner = across(before, swap)
    whole = tuple(
        jnp.where(lead, jnp.concatenate([a, b]), jnp.concatenate([b, a]))
        for a, b in zip(before, partner)
    )
    return jnp.where(lead, whole[1], join(whole, first)[1])


def conv_core(ext_values, weight, free_ext, length):
    tap_count = weight.shape[0]
    summed = jnp.zeros((length,) + ext_values.shape[1:], jnp.float32)
    keeping = jnp.ones((length,), jnp.float32)
    bshape = (length,) + (1,) * (ext_values.ndim - 1)
    for back in range(tap_count):
        if back > 0:
            keeping = keeping * free_ext[tap_count - back : tap_count - back + length]
        sample = ext_values[tap_count - 1 - back : tap_count - 1 - back + length].astype(
            jnp.float32
        )
        summed = summed + weight[tap_count - 1 - back] * sample * keeping.reshape(bshape)
    return jax.nn.silu(summed).astype(jnp.bfloat16)


def body(
    token_values,
    gate_values,
    state_maps,
    step_raw,
    log_rate,
    skip_gain,
    conv_values,
    conv_maps,
    piece_shift,
    doc_start,
    norm_gain,
    out_weight,
):
    owners = lax.axis_size(("dp", "ctx"))
    myself = lax.axis_index(("dp", "ctx"))
    slots = piece_shift.shape[0]
    rows = token_values.shape[1]
    piece_rows = rows // slots
    most = 2 * slots // owners
    slot_ids = jnp.arange(slots, dtype=jnp.int32)
    matching = piece_shift[:, None] == piece_shift[None, :]
    ranking = jnp.sum(
        (matching & (slot_ids[None, :] < slot_ids[:, None])).astype(jnp.int32), axis=1
    )
    offsets = (jnp.arange(owners, dtype=jnp.int32) - myself) % owners
    chosen = (piece_shift[None, None, :] == offsets[:, None, None]) & (
        ranking[None, None, :] == jnp.arange(most, dtype=jnp.int32)[None, :, None]
    )
    send_slot = jnp.sum(chosen.astype(jnp.int32) * slot_ids[None, None, :], axis=2)

    def outgoing(local):
        pieces = local[0].reshape((slots, piece_rows) + local.shape[2:])
        return pieces[send_slot]

    features = token_values.shape[2]
    map_shape = state_maps.shape[2:]
    map_width = map_shape[0] * map_shape[1]
    joined = jnp.concatenate(
        [token_values[0], state_maps[0].reshape(rows, map_width), step_raw[0]], axis=1
    )
    margin = conv_values.shape[0] - 1
    flags = doc_start[0].astype(jnp.bfloat16)
    halo_to = offsets == (piece_shift[slots - 1] + 1) % owners
    flags_to = offsets == 1 % owners
    extra = jnp.concatenate(
        [
            jnp.where(halo_to[:, None, None], joined[None, rows - margin :], 0),
            jnp.where(flags_to[:, None, None], flags[None, rows - margin :, None], 0),
        ],
        axis=2,
    )
    main = outgoing(jnp.concatenate([joined, jnp.zeros_like(flags)[:, None]], axis=1)[None])
    sending = jnp.concatenate(
        [main.reshape((owners, most * piece_rows) + main.shape[3:]), extra], axis=1
    )
    received = lax.all_to_all(sending, ("dp", "ctx"), split_axis=0, concat_axis=0, tiled=True)
    incoming = received[:, : most * piece_rows, :-1].reshape(main.shape[:3] + (-1,))
    incoming_z = lax.all_to_all(
        outgoing(gate_values), ("dp", "ctx"), split_axis=0, concat_axis=0, tiled=True
    )
    source = (myself - piece_shift) % owners

    def placed(received):
        return received[source, ranking].reshape((rows,) + received.shape[3:])

    joined_pack = placed(incoming)
    earlier = lax.axis_index("ctx") > 0
    rim = jnp.concatenate(
        [
            received[(myself - 1 - piece_shift[slots - 1]) % owners, most * piece_rows :, :-1],
            received[(myself - 1) % owners, most * piece_rows :, -1:],
        ],
        axis=1,
    )
    rim = jnp.where(earlier, rim, jnp.zeros_like(rim))
    rim_x = rim[:, :features]
    rim_maps = rim[:, features : features + map_width].reshape((margin,) + map_shape)
    rim_flags = rim[:, -1]
    x_pack = joined_pack[:, :features]
    map_pack = joined_pack[:, features : features + map_width].reshape((rows,) + map_shape)
    dt_pack = joined_pack[:, features + map_width :]
    free_ext = 1.0 - jnp.concatenate([rim_flags, flags]).astype(jnp.float32)
    x_conv = conv_core(jnp.concatenate([rim_x, x_pack]), conv_values, free_ext, rows)
    map_conv = conv_core(jnp.concatenate([rim_maps, map_pack]), conv_maps, free_ext, rows)
    heads_local = log_rate.shape[0]
    groups_local = map_pack.shape[1]
    per_group = heads_local // groups_local
    width = x_pack.shape[1] // heads_local
    state = map_pack.shape[2] // 2
    span = BLOCK_LEN
    blocks = rows // span
    step_dt = jax.nn.softplus(dt_pack.astype(jnp.float32))
    log_decay = step_dt * (-jnp.exp(log_rate))[None, :]
    cum_t = jnp.cumsum(log_decay.reshape(blocks, span, heads_local), axis=1).transpose(0, 2, 1)
    dt_t = step_dt.reshape(blocks, span, heads_local).transpose(0, 2, 1)
    segment = jnp.cumsum(doc_start[0].reshape(blocks, span), axis=1)
    x_blocks = x_conv.reshape(blocks, span, groups_local, per_group, width)
    b_blocks = map_conv[:, :, :state].reshape(blocks, span, groups_local, state)
    c_blocks = map_conv[:, :, state:].reshape(blocks, span, groups_local, state)
    scores = jnp.einsum("bqgn,bsgn->bgqs", c_blocks, b_blocks, preferred_element_type=jnp.float32)
    later = jnp.arange(span)[:, None] >= jnp.arange(span)[None, :]
    allowed = later[None] & (segment[:, :, None] == segment[:, None, :])
    spread = cum_t[:, :, :, None] - cum_t[:, :, None, :]
    decay = jnp.exp(jnp.where(allowed[:, None], spread, -jnp.inf))
    weights = (
        decay.reshape(blocks, groups_local, per_group, span, span)
        * scores[:, :, None]
        * dt_t.reshape(blocks, groups_local, per_group, 1, span)
    ).astype(jnp.bfloat16)
    y_diag = jnp.einsum("bghts,bsghp->btghp", weights, x_blocks, preferred_element_type=jnp.float32)
    same_end = (segment == segment[:, -1:]).astype(jnp.float32)
    carry_coef = jnp.exp(cum_t[:, :, -1:] - cum_t) * dt_t * same_end[:, None, :]
    x_weighted = (
        x_blocks.astype(jnp.float32)
        * carry_coef.transpose(0, 2, 1).reshape(blocks, span, groups_local, per_group, 1)
    ).astype(jnp.bfloat16)
    block_states = jnp.einsum(
        "bsghp,bsgn->bghpn", x_weighted, b_blocks, preferred_element_type=jnp.float32
    ).reshape(blocks, heads_local, width, state)
    block_gates = jnp.exp(cum_t[:, :, -1]) * (segment[:, -1] == 0).astype(jnp.float32)[:, None]

    prior_states = [jnp.zeros_like(block_states[0])]
    prior_gates = [jnp.ones_like(block_gates[0])]
    for b in range(1, blocks):
        prior_states.append(block_gates[b - 1][:, None, None] * prior_states[-1] + block_states[b - 1])
        prior_gates.append(prior_gates[-1] * block_gates[b - 1])
    slab_state = block_gates[-1][:, None, None] * prior_states[-1] + block_states[-1]
    slab_gate = prior_gates[-1] * block_gates[-1]
    z_pack = placed(incoming_z)
    arriving = chain(slab_gate, slab_state, "ctx")
    entering = (
        (jnp.stack(prior_states) + jnp.stack(prior_gates)[:, :, None, None] * arriving[None])
        .astype(jnp.bfloat16)
        .reshape(blocks, groups_local, per_group, width, state)
    )
    y_off = jnp.einsum("bqgn,bghpn->bqghp", c_blocks, entering, preferred_element_type=jnp.float32)
    reach = (
        (jnp.exp(cum_t) * (segment == 0).astype(jnp.float32)[:, None, :])
        .transpose(0, 2, 1)
        .reshape(blocks, span, groups_local, per_group, 1)
    )
    mixed_y = (
        y_diag
        + y_off * reach
        + skip_gain.reshape(groups_local, per_group, 1) * x_blocks.astype(jnp.float32)
    )
    gated = mixed_y * jax.nn.silu(
        z_pack.astype(jnp.float32).reshape(blocks, span, groups_local, per_group, width)
    )
    power = jnp.mean(gated * gated, axis=(3, 4), keepdims=True)
    normed = (
        (gated * lax.rsqrt(power + eps) * norm_gain.reshape(groups_local, per_group, width))
        .astype(jnp.bfloat16)
        .reshape(rows, heads_local * width)
    )
    partial_value = jnp.dot(normed, out_weight, preferred_element_type=jnp.float32)
    result = lax.psum_scatter(
        partial_value.astype(jnp.bfloat16), "head", scatter_dimension=1, tiled=True
    )
    return result[None]


def solution(mesh):
    return jax.shard_map(
        body,
        mesh=mesh,
        in_specs=(
            P("dp", "ctx", "head"),
            P("dp", "ctx", "head"),
            P("dp", "ctx", "head", None),
            P("dp", "ctx", "head"),
            P("head"),
            P("head"),
            P(None, "head"),
            P(None, "head", None),
            P(),
            P("dp", "ctx"),
            P("head"),
            P("head", None),
        ),
        out_specs=P("dp", "ctx", "head"),
        check_vma=False,
    )
```

```python
import jax
import jax.numpy as jnp
from jax import lax
from jax.sharding import PartitionSpec as P

BLOCK_LEN = 128


eps = 1e-05


def passed_along(block, axis, distance):
    devices = range(lax.axis_size(axis))
    route = [(i - distance, i) for i in devices if i - distance in devices]
    return lax.ppermute(block, axis, route)


def chain(gate, summed, axis):
    count = lax.axis_size(axis)
    place = lax.axis_index(axis)
    core = place % 2
    chip = place // 2
    chips = count // 2
    swap = [(i, i ^ 1) for i in range(count)]

    def join(earlier, latter):
        return (earlier[0] * latter[0], latter[0][:, None, None] * earlier[1] + latter[1])

    def across(pair, route):
        gate_in, summed_in = lax.ppermute((pair[0], pair[1].astype(jnp.bfloat16)), axis, route)
        return gate_in, summed_in.astype(jnp.float32)

    local = (gate, summed)
    other = across(local, swap)
    lead = core == 0
    first = tuple(jnp.where(lead, a, b) for a, b in zip(local, other))
    second = tuple(jnp.where(lead, b, a) for a, b in zip(local, other))
    both = join(first, second)
    half = gate.shape[0] // 2
    mine = tuple(lax.dynamic_slice_in_dim(a, core * half, half, 0) for a in both)

    def fetch(pair, distance):
        gate_in, summed_in = across(pair, [(i - 2 * distance, i) for i in range(2 * distance, count)])
        return jnp.where(chip >= distance, gate_in, 1.0), summed_in

    before = fetch(mine, 1)
    window = join(before, mine)
    distance = 2
    while distance < chips:
        received = fetch(window, distance)
        before = join(received, before)
        distance *= 2
        if distance < chips:
            window = join(received, window)
    partner = across(before, swap)
    whole = tuple(
        jnp.where(lead, jnp.concatenate([a, b]), jnp.concatenate([b, a]))
        for a, b in zip(before, partner)
    )
    return jnp.where(lead, whole[1], join(whole, first)[1])


def conv_core(ext_values, weight, free_ext, length):
    tap_count = weight.shape[0]
    summed = jnp.zeros((length,) + ext_values.shape[1:], jnp.float32)
    keeping = jnp.ones((length,), jnp.float32)
    bshape = (length,) + (1,) * (ext_values.ndim - 1)
    for back in range(tap_count):
        if back > 0:
            keeping = keeping * free_ext[tap_count - back : tap_count - back + length]
        sample = ext_values[tap_count - 1 - back : tap_count - 1 - back + length].astype(
            jnp.float32
        )
        summed = summed + weight[tap_count - 1 - back] * sample * keeping.reshape(bshape)
    return jax.nn.silu(summed).astype(jnp.bfloat16)


def body(
    token_values,
    gate_values,
    state_maps,
    step_raw,
    log_rate,
    skip_gain,
    conv_values,
    conv_maps,
    piece_shift,
    doc_start,
    norm_gain,
    out_weight,
):
    owners = lax.axis_size(("dp", "ctx"))
    myself = lax.axis_index(("dp", "ctx"))
    slots = piece_shift.shape[0]
    rows = token_values.shape[1]
    piece_rows = rows // slots
    most = 2 * slots // owners
    slot_ids = jnp.arange(slots, dtype=jnp.int32)
    matching = piece_shift[:, None] == piece_shift[None, :]
    ranking = jnp.sum(
        (matching & (slot_ids[None, :] < slot_ids[:, None])).astype(jnp.int32), axis=1
    )
    offsets = (jnp.arange(owners, dtype=jnp.int32) - myself) % owners
    chosen = (piece_shift[None, None, :] == offsets[:, None, None]) & (
        ranking[None, None, :] == jnp.arange(most, dtype=jnp.int32)[None, :, None]
    )
    send_slot = jnp.sum(chosen.astype(jnp.int32) * slot_ids[None, None, :], axis=2)

    def outgoing(local):
        pieces = local[0].reshape((slots, piece_rows) + local.shape[2:])
        return pieces[send_slot]

    features = token_values.shape[2]
    map_shape = state_maps.shape[2:]
    map_width = map_shape[0] * map_shape[1]
    joined = jnp.concatenate(
        [token_values[0], state_maps[0].reshape(rows, map_width), step_raw[0]], axis=1
    )
    incoming = lax.all_to_all(
        outgoing(joined[None]), ("dp", "ctx"), split_axis=0, concat_axis=0, tiled=True
    )
    incoming_z = lax.all_to_all(
        outgoing(gate_values), ("dp", "ctx"), split_axis=0, concat_axis=0, tiled=True
    )
    source = (myself - piece_shift) % owners

    def placed(received):
        return received[source, ranking].reshape((rows,) + received.shape[3:])

    joined_pack = placed(incoming)
    margin = conv_values.shape[0] - 1
    flags = doc_start[0].astype(jnp.bfloat16)
    def shifter(distance):
        if distance == 0:
            return lambda block: block
        route = [(i, (i + distance) % owners) for i in range(owners)]
        return lambda block: lax.ppermute(block, ("dp", "ctx"), route)

    halo = lax.switch(
        (piece_shift[slots - 1] + 1) % owners,
        [shifter(distance) for distance in range(owners)],
        joined[rows - margin :],
    )
    earlier = lax.axis_index("ctx") > 0
    rim = jnp.concatenate(
        [halo, passed_along(flags[rows - margin :], "ctx", 1)[:, None]], axis=1
    )
    rim = jnp.where(earlier, rim, jnp.zeros_like(rim))
    rim_x = rim[:, :features]
    rim_maps = rim[:, features : features + map_width].reshape((margin,) + map_shape)
    rim_flags = rim[:, -1]
    x_pack = joined_pack[:, :features]
    map_pack = joined_pack[:, features : features + map_width].reshape((rows,) + map_shape)
    dt_pack = joined_pack[:, features + map_width :]
    free_ext = 1.0 - jnp.concatenate([rim_flags, flags]).astype(jnp.float32)
    x_conv = conv_core(jnp.concatenate([rim_x, x_pack]), conv_values, free_ext, rows)
    map_conv = conv_core(jnp.concatenate([rim_maps, map_pack]), conv_maps, free_ext, rows)
    heads_local = log_rate.shape[0]
    groups_local = map_pack.shape[1]
    per_group = heads_local // groups_local
    width = x_pack.shape[1] // heads_local
    state = map_pack.shape[2] // 2
    span = BLOCK_LEN
    blocks = rows // span
    step_dt = jax.nn.softplus(dt_pack.astype(jnp.float32))
    log_decay = step_dt * (-jnp.exp(log_rate))[None, :]
    cum_t = jnp.cumsum(log_decay.reshape(blocks, span, heads_local), axis=1).transpose(0, 2, 1)
    dt_t = step_dt.reshape(blocks, span, heads_local).transpose(0, 2, 1)
    segment = jnp.cumsum(doc_start[0].reshape(blocks, span), axis=1)
    x_blocks = x_conv.reshape(blocks, span, groups_local, per_group, width)
    b_blocks = map_conv[:, :, :state].reshape(blocks, span, groups_local, state)
    c_blocks = map_conv[:, :, state:].reshape(blocks, span, groups_local, state)
    scores = jnp.einsum("bqgn,bsgn->bgqs", c_blocks, b_blocks, preferred_element_type=jnp.float32)
    later = jnp.arange(span)[:, None] >= jnp.arange(span)[None, :]
    allowed = later[None] & (segment[:, :, None] == segment[:, None, :])
    spread = cum_t[:, :, :, None] - cum_t[:, :, None, :]
    decay = jnp.exp(jnp.where(allowed[:, None], spread, -jnp.inf))
    weights = (
        decay.reshape(blocks, groups_local, per_group, span, span)
        * scores[:, :, None]
        * dt_t.reshape(blocks, groups_local, per_group, 1, span)
    ).astype(jnp.bfloat16)
    y_diag = jnp.einsum("bghts,bsghp->btghp", weights, x_blocks, preferred_element_type=jnp.float32)
    same_end = (segment == segment[:, -1:]).astype(jnp.float32)
    carry_coef = jnp.exp(cum_t[:, :, -1:] - cum_t) * dt_t * same_end[:, None, :]
    x_weighted = (
        x_blocks.astype(jnp.float32)
        * carry_coef.transpose(0, 2, 1).reshape(blocks, span, groups_local, per_group, 1)
    ).astype(jnp.bfloat16)
    block_states = jnp.einsum(
        "bsghp,bsgn->bghpn", x_weighted, b_blocks, preferred_element_type=jnp.float32
    ).reshape(blocks, heads_local, width, state)
    block_gates = jnp.exp(cum_t[:, :, -1]) * (segment[:, -1] == 0).astype(jnp.float32)[:, None]

    prior_states = [jnp.zeros_like(block_states[0])]
    prior_gates = [jnp.ones_like(block_gates[0])]
    for b in range(1, blocks):
        prior_states.append(block_gates[b - 1][:, None, None] * prior_states[-1] + block_states[b - 1])
        prior_gates.append(prior_gates[-1] * block_gates[b - 1])
    slab_state = block_gates[-1][:, None, None] * prior_states[-1] + block_states[-1]
    slab_gate = prior_gates[-1] * block_gates[-1]
    z_pack = placed(incoming_z)
    arriving = chain(slab_gate, slab_state, "ctx")
    entering = (
        (jnp.stack(prior_states) + jnp.stack(prior_gates)[:, :, None, None] * arriving[None])
        .astype(jnp.bfloat16)
        .reshape(blocks, groups_local, per_group, width, state)
    )
    y_off = jnp.einsum("bqgn,bghpn->bqghp", c_blocks, entering, preferred_element_type=jnp.float32)
    reach = (
        (jnp.exp(cum_t) * (segment == 0).astype(jnp.float32)[:, None, :])
        .transpose(0, 2, 1)
        .reshape(blocks, span, groups_local, per_group, 1)
    )
    mixed_y = (
        y_diag
        + y_off * reach
        + skip_gain.reshape(groups_local, per_group, 1) * x_blocks.astype(jnp.float32)
    )
    gated = mixed_y * jax.nn.silu(
        z_pack.astype(jnp.float32).reshape(blocks, span, groups_local, per_group, width)
    )
    power = jnp.mean(gated * gated, axis=(3, 4), keepdims=True)
    normed = (
        (gated * lax.rsqrt(power + eps) * norm_gain.reshape(groups_local, per_group, width))
        .astype(jnp.bfloat16)
        .reshape(rows, heads_local * width)
    )
    partial_value = jnp.dot(normed, out_weight, preferred_element_type=jnp.float32)
    result = lax.psum_scatter(
        partial_value.astype(jnp.bfloat16), "head", scatter_dimension=1, tiled=True
    )
    return result[None]


def solution(mesh):
    return jax.shard_map(
        body,
        mesh=mesh,
        in_specs=(
            P("dp", "ctx", "head"),
            P("dp", "ctx", "head"),
            P("dp", "ctx", "head", None),
            P("dp", "ctx", "head"),
            P("head"),
            P("head"),
            P(None, "head"),
            P(None, "head", None),
            P(),
            P("dp", "ctx"),
            P("head"),
            P("head", None),
        ),
        out_specs=P("dp", "ctx", "head"),
        check_vma=False,
    )
```

```python
import jax
import jax.numpy as jnp
from jax import lax
from jax.sharding import PartitionSpec as P

BLOCK_LEN = 128


eps = 1e-05


def passed_along(block, axis, distance):
    devices = range(lax.axis_size(axis))
    route = [(i - distance, i) for i in devices if i - distance in devices]
    return lax.ppermute(block, axis, route)


def chain(gate, summed, axis):
    count = lax.axis_size(axis)
    place = lax.axis_index(axis)
    core = place % 2
    chip = place // 2
    chips = count // 2
    swap = [(i, i ^ 1) for i in range(count)]

    def join(earlier, latter):
        return (earlier[0] * latter[0], latter[0][:, None, None] * earlier[1] + latter[1])

    def across(pair, route):
        gate_in, summed_in = lax.ppermute((pair[0], pair[1].astype(jnp.bfloat16)), axis, route)
        return gate_in, summed_in.astype(jnp.float32)

    local = (gate, summed)
    other = across(local, swap)
    lead = core == 0
    first = tuple(jnp.where(lead, a, b) for a, b in zip(local, other))
    second = tuple(jnp.where(lead, b, a) for a, b in zip(local, other))
    both = join(first, second)
    half = gate.shape[0] // 2
    mine = tuple(lax.dynamic_slice_in_dim(a, core * half, half, 0) for a in both)

    def fetch(pair, distance):
        gate_in, summed_in = across(pair, [(i - 2 * distance, i) for i in range(2 * distance, count)])
        return jnp.where(chip >= distance, gate_in, 1.0), summed_in

    before = fetch(mine, 1)
    window = join(before, mine)
    distance = 2
    while distance < chips:
        received = fetch(window, distance)
        before = join(received, before)
        distance *= 2
        if distance < chips:
            window = join(received, window)
    partner = across(before, swap)
    whole = tuple(
        jnp.where(lead, jnp.concatenate([a, b]), jnp.concatenate([b, a]))
        for a, b in zip(before, partner)
    )
    return jnp.where(lead, whole[1], join(whole, first)[1])


def conv_core(ext_values, weight, free_ext, length):
    tap_count = weight.shape[0]
    summed = jnp.zeros((length,) + ext_values.shape[1:], jnp.float32)
    keeping = jnp.ones((length,), jnp.float32)
    bshape = (length,) + (1,) * (ext_values.ndim - 1)
    for back in range(tap_count):
        if back > 0:
            keeping = keeping * free_ext[tap_count - back : tap_count - back + length]
        sample = ext_values[tap_count - 1 - back : tap_count - 1 - back + length].astype(
            jnp.float32
        )
        summed = summed + weight[tap_count - 1 - back] * sample * keeping.reshape(bshape)
    return jax.nn.silu(summed).astype(jnp.bfloat16)


def body(
    token_values,
    gate_values,
    state_maps,
    step_raw,
    log_rate,
    skip_gain,
    conv_values,
    conv_maps,
    piece_shift,
    doc_start,
    norm_gain,
    out_weight,
):
    owners = lax.axis_size(("dp", "ctx"))
    myself = lax.axis_index(("dp", "ctx"))
    slots = piece_shift.shape[0]
    rows = token_values.shape[1]
    piece_rows = rows // slots
    most = 2 * slots // owners
    slot_ids = jnp.arange(slots, dtype=jnp.int32)
    matching = piece_shift[:, None] == piece_shift[None, :]
    ranking = jnp.sum(
        (matching & (slot_ids[None, :] < slot_ids[:, None])).astype(jnp.int32), axis=1
    )
    offsets = (jnp.arange(owners, dtype=jnp.int32) - myself) % owners
    chosen = (piece_shift[None, None, :] == offsets[:, None, None]) & (
        ranking[None, None, :] == jnp.arange(most, dtype=jnp.int32)[None, :, None]
    )
    send_slot = jnp.sum(chosen.astype(jnp.int32) * slot_ids[None, None, :], axis=2)

    def outgoing(local):
        pieces = local[0].reshape((slots, piece_rows) + local.shape[2:])
        return pieces[send_slot]

    features = token_values.shape[2]
    map_shape = state_maps.shape[2:]
    map_width = map_shape[0] * map_shape[1]
    joined = jnp.concatenate(
        [token_values[0], state_maps[0].reshape(rows, map_width), step_raw[0]], axis=1
    )
    incoming = lax.all_to_all(
        outgoing(joined[None]), ("dp", "ctx"), split_axis=0, concat_axis=0, tiled=True
    )
    incoming_z = lax.all_to_all(
        outgoing(gate_values), ("dp", "ctx"), split_axis=0, concat_axis=0, tiled=True
    )
    source = (myself - piece_shift) % owners

    def placed(received):
        return received[source, ranking].reshape((rows,) + received.shape[3:])

    joined_pack = placed(incoming)
    margin = conv_values.shape[0] - 1
    flags = doc_start[0].astype(jnp.bfloat16)
    halo = joined[rows - margin :]
    halo_shift = (piece_shift[slots - 1] + 1) % owners
    distance = 1
    while distance < owners:
        route = [(i, (i + distance) % owners) for i in range(owners)]
        halo = lax.cond(
            (halo_shift // distance) % 2 == 1,
            lambda block, route=route: lax.ppermute(block, ("dp", "ctx"), route),
            lambda block: block,
            halo,
        )
        distance *= 2
    earlier = lax.axis_index("ctx") > 0
    rim = jnp.concatenate(
        [halo, passed_along(flags[rows - margin :], "ctx", 1)[:, None]], axis=1
    )
    rim = jnp.where(earlier, rim, jnp.zeros_like(rim))
    rim_x = rim[:, :features]
    rim_maps = rim[:, features : features + map_width].reshape((margin,) + map_shape)
    rim_flags = rim[:, -1]
    x_pack = joined_pack[:, :features]
    map_pack = joined_pack[:, features : features + map_width].reshape((rows,) + map_shape)
    dt_pack = joined_pack[:, features + map_width :]
    free_ext = 1.0 - jnp.concatenate([rim_flags, flags]).astype(jnp.float32)
    x_conv = conv_core(jnp.concatenate([rim_x, x_pack]), conv_values, free_ext, rows)
    map_conv = conv_core(jnp.concatenate([rim_maps, map_pack]), conv_maps, free_ext, rows)
    heads_local = log_rate.shape[0]
    groups_local = map_pack.shape[1]
    per_group = heads_local // groups_local
    width = x_pack.shape[1] // heads_local
    state = map_pack.shape[2] // 2
    span = BLOCK_LEN
    blocks = rows // span
    step_dt = jax.nn.softplus(dt_pack.astype(jnp.float32))
    log_decay = step_dt * (-jnp.exp(log_rate))[None, :]
    cum_t = jnp.cumsum(log_decay.reshape(blocks, span, heads_local), axis=1).transpose(0, 2, 1)
    dt_t = step_dt.reshape(blocks, span, heads_local).transpose(0, 2, 1)
    segment = jnp.cumsum(doc_start[0].reshape(blocks, span), axis=1)
    x_blocks = x_conv.reshape(blocks, span, groups_local, per_group, width)
    b_blocks = map_conv[:, :, :state].reshape(blocks, span, groups_local, state)
    c_blocks = map_conv[:, :, state:].reshape(blocks, span, groups_local, state)
    scores = jnp.einsum("bqgn,bsgn->bgqs", c_blocks, b_blocks, preferred_element_type=jnp.float32)
    later = jnp.arange(span)[:, None] >= jnp.arange(span)[None, :]
    allowed = later[None] & (segment[:, :, None] == segment[:, None, :])
    spread = cum_t[:, :, :, None] - cum_t[:, :, None, :]
    decay = jnp.exp(jnp.where(allowed[:, None], spread, -jnp.inf))
    weights = (
        decay.reshape(blocks, groups_local, per_group, span, span)
        * scores[:, :, None]
        * dt_t.reshape(blocks, groups_local, per_group, 1, span)
    ).astype(jnp.bfloat16)
    y_diag = jnp.einsum("bghts,bsghp->btghp", weights, x_blocks, preferred_element_type=jnp.float32)
    same_end = (segment == segment[:, -1:]).astype(jnp.float32)
    carry_coef = jnp.exp(cum_t[:, :, -1:] - cum_t) * dt_t * same_end[:, None, :]
    x_weighted = (
        x_blocks.astype(jnp.float32)
        * carry_coef.transpose(0, 2, 1).reshape(blocks, span, groups_local, per_group, 1)
    ).astype(jnp.bfloat16)
    block_states = jnp.einsum(
        "bsghp,bsgn->bghpn", x_weighted, b_blocks, preferred_element_type=jnp.float32
    ).reshape(blocks, heads_local, width, state)
    block_gates = jnp.exp(cum_t[:, :, -1]) * (segment[:, -1] == 0).astype(jnp.float32)[:, None]

    prior_states = [jnp.zeros_like(block_states[0])]
    prior_gates = [jnp.ones_like(block_gates[0])]
    for b in range(1, blocks):
        prior_states.append(block_gates[b - 1][:, None, None] * prior_states[-1] + block_states[b - 1])
        prior_gates.append(prior_gates[-1] * block_gates[b - 1])
    slab_state = block_gates[-1][:, None, None] * prior_states[-1] + block_states[-1]
    slab_gate = prior_gates[-1] * block_gates[-1]
    z_pack = placed(incoming_z)
    arriving = chain(slab_gate, slab_state, "ctx")
    entering = (
        (jnp.stack(prior_states) + jnp.stack(prior_gates)[:, :, None, None] * arriving[None])
        .astype(jnp.bfloat16)
        .reshape(blocks, groups_local, per_group, width, state)
    )
    y_off = jnp.einsum("bqgn,bghpn->bqghp", c_blocks, entering, preferred_element_type=jnp.float32)
    reach = (
        (jnp.exp(cum_t) * (segment == 0).astype(jnp.float32)[:, None, :])
        .transpose(0, 2, 1)
        .reshape(blocks, span, groups_local, per_group, 1)
    )
    mixed_y = (
        y_diag
        + y_off * reach
        + skip_gain.reshape(groups_local, per_group, 1) * x_blocks.astype(jnp.float32)
    )
    gated = mixed_y * jax.nn.silu(
        z_pack.astype(jnp.float32).reshape(blocks, span, groups_local, per_group, width)
    )
    power = jnp.mean(gated * gated, axis=(3, 4), keepdims=True)
    normed = (
        (gated * lax.rsqrt(power + eps) * norm_gain.reshape(groups_local, per_group, width))
        .astype(jnp.bfloat16)
        .reshape(rows, heads_local * width)
    )
    partial_value = jnp.dot(normed, out_weight, preferred_element_type=jnp.float32)
    result = lax.psum_scatter(
        partial_value.astype(jnp.bfloat16), "head", scatter_dimension=1, tiled=True
    )
    return result[None]


def solution(mesh):
    return jax.shard_map(
        body,
        mesh=mesh,
        in_specs=(
            P("dp", "ctx", "head"),
            P("dp", "ctx", "head"),
            P("dp", "ctx", "head", None),
            P("dp", "ctx", "head"),
            P("head"),
            P("head"),
            P(None, "head"),
            P(None, "head", None),
            P(),
            P("dp", "ctx"),
            P("head"),
            P("head", None),
        ),
        out_specs=P("dp", "ctx", "head"),
        check_vma=False,
    )
```

```python
import jax
import jax.numpy as jnp
from jax import lax
from jax.sharding import PartitionSpec as P

BLOCK_LEN = 128


eps = 1e-05


def passed_along(block, axis, distance):
    devices = range(lax.axis_size(axis))
    route = [(i - distance, i) for i in devices if i - distance in devices]
    return lax.ppermute(block, axis, route)


def chain(gate, summed, axis):
    count = lax.axis_size(axis)
    place = lax.axis_index(axis)
    core = place % 2
    chip = place // 2
    chips = count // 2
    swap = [(i, i ^ 1) for i in range(count)]

    def join(earlier, latter):
        return (earlier[0] * latter[0], latter[0][:, None, None] * earlier[1] + latter[1])

    def across(pair, route):
        gate_in, summed_in = lax.ppermute((pair[0], pair[1].astype(jnp.bfloat16)), axis, route)
        return gate_in, summed_in.astype(jnp.float32)

    local = (gate, summed)
    other = across(local, swap)
    lead = core == 0
    first = tuple(jnp.where(lead, a, b) for a, b in zip(local, other))
    second = tuple(jnp.where(lead, b, a) for a, b in zip(local, other))
    both = join(first, second)
    half = gate.shape[0] // 2
    mine = tuple(lax.dynamic_slice_in_dim(a, core * half, half, 0) for a in both)

    def fetch(pair, distance):
        gate_in, summed_in = across(pair, [(i - 2 * distance, i) for i in range(2 * distance, count)])
        return jnp.where(chip >= distance, gate_in, 1.0), summed_in

    before = fetch(mine, 1)
    window = join(before, mine)
    distance = 2
    while distance < chips:
        received = fetch(window, distance)
        before = join(received, before)
        distance *= 2
        if distance < chips:
            window = join(received, window)
    partner = across(before, swap)
    whole = tuple(
        jnp.where(lead, jnp.concatenate([a, b]), jnp.concatenate([b, a]))
        for a, b in zip(before, partner)
    )
    return jnp.where(lead, whole[1], join(whole, first)[1])


def conv_core(ext_values, weight, free_ext, length):
    tap_count = weight.shape[0]
    summed = jnp.zeros((length,) + ext_values.shape[1:], jnp.float32)
    keeping = jnp.ones((length,), jnp.float32)
    bshape = (length,) + (1,) * (ext_values.ndim - 1)
    for back in range(tap_count):
        if back > 0:
            keeping = keeping * free_ext[tap_count - back : tap_count - back + length]
        sample = ext_values[tap_count - 1 - back : tap_count - 1 - back + length].astype(
            jnp.float32
        )
        summed = summed + weight[tap_count - 1 - back] * sample * keeping.reshape(bshape)
    return jax.nn.silu(summed).astype(jnp.bfloat16)


def body(
    token_values,
    gate_values,
    state_maps,
    step_raw,
    log_rate,
    skip_gain,
    conv_values,
    conv_maps,
    piece_shift,
    doc_start,
    norm_gain,
    out_weight,
):
    owners = lax.axis_size(("dp", "ctx"))
    myself = lax.axis_index(("dp", "ctx"))
    slots = piece_shift.shape[0]
    rows = token_values.shape[1]
    piece_rows = rows // slots
    most = 2 * slots // owners
    slot_ids = jnp.arange(slots, dtype=jnp.int32)
    matching = piece_shift[:, None] == piece_shift[None, :]
    ranking = jnp.sum(
        (matching & (slot_ids[None, :] < slot_ids[:, None])).astype(jnp.int32), axis=1
    )
    offsets = (jnp.arange(owners, dtype=jnp.int32) - myself) % owners
    chosen = (piece_shift[None, None, :] == offsets[:, None, None]) & (
        ranking[None, None, :] == jnp.arange(most, dtype=jnp.int32)[None, :, None]
    )
    send_slot = jnp.sum(chosen.astype(jnp.int32) * slot_ids[None, None, :], axis=2)

    def outgoing(local):
        pieces = local[0].reshape((slots, piece_rows) + local.shape[2:])
        return pieces[send_slot]

    features = token_values.shape[2]
    map_shape = state_maps.shape[2:]
    map_width = map_shape[0] * map_shape[1]
    joined = jnp.concatenate(
        [token_values[0], state_maps[0].reshape(rows, map_width), step_raw[0]], axis=1
    )
    incoming = lax.all_to_all(
        outgoing(joined[None]), ("dp", "ctx"), split_axis=0, concat_axis=0, tiled=True
    )
    incoming_z = lax.all_to_all(
        outgoing(gate_values), ("dp", "ctx"), split_axis=0, concat_axis=0, tiled=True
    )
    source = (myself - piece_shift) % owners

    def placed(received):
        return received[source, ranking].reshape((rows,) + received.shape[3:])

    joined_pack = placed(incoming)
    margin = conv_values.shape[0] - 1
    flags = doc_start[0].astype(jnp.bfloat16)
    halo = joined[rows - margin :]
    halo_shift = (piece_shift[slots - 1] + 1) % owners
    distance = 1
    while distance < owners:
        route = [(i, (i + distance) % owners) for i in range(owners)]
        halo = lax.cond(
            (halo_shift // distance) % 2 == 1,
            lambda block, route=route: lax.ppermute(block, ("dp", "ctx"), route),
            lambda block: block,
            halo,
        )
        distance *= 2
    earlier = lax.axis_index("ctx") > 0
    rim = jnp.concatenate(
        [halo, passed_along(flags[rows - margin :], "ctx", 1)[:, None]], axis=1
    )
    rim = jnp.where(earlier, rim, jnp.zeros_like(rim))
    rim_x = rim[:, :features]
    rim_maps = rim[:, features : features + map_width].reshape((margin,) + map_shape)
    rim_flags = rim[:, -1]
    x_pack = joined_pack[:, :features]
    map_pack = joined_pack[:, features : features + map_width].reshape((rows,) + map_shape)
    dt_pack = joined_pack[:, features + map_width :]
    free_ext = 1.0 - jnp.concatenate([rim_flags, flags]).astype(jnp.float32)
    x_conv = conv_core(jnp.concatenate([rim_x, x_pack]), conv_values, free_ext, rows)
    map_conv = conv_core(jnp.concatenate([rim_maps, map_pack]), conv_maps, free_ext, rows)
    heads_local = log_rate.shape[0]
    groups_local = map_pack.shape[1]
    per_group = heads_local // groups_local
    width = x_pack.shape[1] // heads_local
    state = map_pack.shape[2] // 2
    span = BLOCK_LEN
    blocks = rows // span
    step_dt = jax.nn.softplus(dt_pack.astype(jnp.float32))
    log_decay = step_dt * (-jnp.exp(log_rate))[None, :]
    cum_t = jnp.cumsum(log_decay.reshape(blocks, span, heads_local), axis=1).transpose(0, 2, 1)
    dt_t = step_dt.reshape(blocks, span, heads_local).transpose(0, 2, 1)
    segment = jnp.cumsum(doc_start[0].reshape(blocks, span), axis=1)
    x_blocks = x_conv.reshape(blocks, span, groups_local, per_group, width)
    b_blocks = map_conv[:, :, :state].reshape(blocks, span, groups_local, state)
    c_blocks = map_conv[:, :, state:].reshape(blocks, span, groups_local, state)
    scores = jnp.einsum("bqgn,bsgn->bgqs", c_blocks, b_blocks, preferred_element_type=jnp.float32)
    later = jnp.arange(span)[:, None] >= jnp.arange(span)[None, :]
    allowed = later[None] & (segment[:, :, None] == segment[:, None, :])
    spread = cum_t[:, :, :, None] - cum_t[:, :, None, :]
    decay = jnp.exp(jnp.where(allowed[:, None], spread, -jnp.inf))
    weights = (
        decay.reshape(blocks, groups_local, per_group, span, span)
        * scores[:, :, None]
        * dt_t.reshape(blocks, groups_local, per_group, 1, span)
    ).astype(jnp.bfloat16)
    y_diag = jnp.einsum("bghts,bsghp->btghp", weights, x_blocks, preferred_element_type=jnp.float32)
    same_end = (segment == segment[:, -1:]).astype(jnp.float32)
    carry_coef = jnp.exp(cum_t[:, :, -1:] - cum_t) * dt_t * same_end[:, None, :]
    x_weighted = (
        x_blocks.astype(jnp.float32)
        * carry_coef.transpose(0, 2, 1).reshape(blocks, span, groups_local, per_group, 1)
    ).astype(jnp.bfloat16)
    block_states = jnp.einsum(
        "bsghp,bsgn->bghpn", x_weighted, b_blocks, preferred_element_type=jnp.float32
    ).reshape(blocks, heads_local, width, state)
    block_gates = jnp.exp(cum_t[:, :, -1]) * (segment[:, -1] == 0).astype(jnp.float32)[:, None]

    prior_states = [jnp.zeros_like(block_states[0])]
    prior_gates = [jnp.ones_like(block_gates[0])]
    for b in range(1, blocks):
        prior_states.append(block_gates[b - 1][:, None, None] * prior_states[-1] + block_states[b - 1])
        prior_gates.append(prior_gates[-1] * block_gates[b - 1])
    slab_state = block_gates[-1][:, None, None] * prior_states[-1] + block_states[-1]
    slab_gate = prior_gates[-1] * block_gates[-1]
    z_pack = placed(incoming_z)
    arriving = chain(slab_gate, slab_state, "ctx")
    entering = (
        (jnp.stack(prior_states) + jnp.stack(prior_gates)[:, :, None, None] * arriving[None])
        .astype(jnp.bfloat16)
        .reshape(blocks, groups_local, per_group, width, state)
    )
    y_off = jnp.einsum("bqgn,bghpn->bqghp", c_blocks, entering, preferred_element_type=jnp.float32)
    reach = (
        (jnp.exp(cum_t) * (segment == 0).astype(jnp.float32)[:, None, :])
        .transpose(0, 2, 1)
        .reshape(blocks, span, groups_local, per_group, 1)
    )
    ready_y = y_diag + skip_gain.reshape(groups_local, per_group, 1) * x_blocks.astype(jnp.float32)
    gate_act = jax.nn.silu(
        z_pack.astype(jnp.float32).reshape(blocks, span, groups_local, per_group, width)
    )
    ready_y, gate_act = lax.optimization_barrier((ready_y, gate_act))
    gated = (ready_y + y_off * reach) * gate_act
    power = jnp.mean(gated * gated, axis=(3, 4), keepdims=True)
    normed = (
        (gated * lax.rsqrt(power + eps) * norm_gain.reshape(groups_local, per_group, width))
        .astype(jnp.bfloat16)
        .reshape(rows, heads_local * width)
    )
    partial_value = jnp.dot(normed, out_weight, preferred_element_type=jnp.float32)
    result = lax.psum_scatter(
        partial_value.astype(jnp.bfloat16), "head", scatter_dimension=1, tiled=True
    )
    return result[None]


def solution(mesh):
    return jax.shard_map(
        body,
        mesh=mesh,
        in_specs=(
            P("dp", "ctx", "head"),
            P("dp", "ctx", "head"),
            P("dp", "ctx", "head", None),
            P("dp", "ctx", "head"),
            P("head"),
            P("head"),
            P(None, "head"),
            P(None, "head", None),
            P(),
            P("dp", "ctx"),
            P("head"),
            P("head", None),
        ),
        out_specs=P("dp", "ctx", "head"),
        check_vma=False,
    )
```
